128 devices in a mesh: dp: 4 (over z), rows: 32 (over y, x, core).
Axes of the slice: x: 4, y: 4, z: 4, core: 2. Of those that a mesh axis runs over, the one named last changes fastest.
Arguments:
- images: bfloat16 [4, 64, 256, 2048], P('dp', None, 'rows'), may hold values from -1000 to 1000
- conv_w: float32 [576, 64], replicated, may hold values from -0.25 to 0.25
- bias: float32 [64], replicated, may hold values from -4 to 4
- cotangent: bfloat16 [4, 64, 256, 2048], P('dp', None, 'rows'), may hold values from -1500 to 1500
Outputs:
- outputs: bfloat16 [4, 64, 256, 2048], P('dp', None, 'rows')
- grad_x: bfloat16 [4, 64, 256, 2048], P('dp', None, 'rows')
- grad_w: float32 [576, 64], replicated
The draws below stay inside these ranges and needn't reach their ends.
All inputs are finite; a program needn't handle non-finite values.
Results may differ from the reference program's by a relative error of at most 0.0017.
The reference program's roundings to bfloat16 on the way (of `patches` and `mixing_b`) count: a program that leaves them out, or rounds other values in their place, can miss the bound.
Values may be sent and summed in bfloat16 or wider, within the bound.
No kernel may reach another device: no remote copies, remote signals or barrier semaphores. Data moves between devices by JAX's collectives and lax.ppermute only.
A program may use at most 128 MiB of HBM per device.

```python
import jax
import jax.numpy as jnp
from jax import lax

C = 64
PATCH = 576
IW = 2048
ITERS = 5
BATCH = 4
HEIGHT = 256


def base_fields(key):
    noise_key = jax.random.fold_in(key, 11)
    first_key, second_key = jax.random.split(noise_key)
    field = jnp.clip(jax.random.normal(first_key, (BATCH, C, HEIGHT, IW), jnp.float32), -3.0, 3.0)
    common = jnp.clip(jax.random.normal(second_key, (BATCH, 1, HEIGHT, IW), jnp.float32), -3.0, 3.0)
    return (field, common)


def height_pos():
    return jnp.arange(HEIGHT, dtype=jnp.float32).reshape(1, 1, HEIGHT, 1) / max(HEIGHT - 1, 1)


def height_ramp():
    ramp_factor = 1.0 + 2.0 * height_pos()
    return ramp_factor


def steep_ramp():
    ramp_factor = 3.0 - 2.0 * height_pos()
    return ramp_factor


def draw_images(key, part):
    field, common = base_fields(key)
    own_key = jax.random.fold_in(key, 23)
    key_scale, key_mix, key_gain = jax.random.split(own_key, 3)
    scales = jnp.exp(jax.random.uniform(key_scale, (1, C, 1, 1), jnp.float32, 0.0, jnp.log(4.0)))
    mixes = jax.random.uniform(key_mix, (1, C, 1, 1), jnp.float32, -0.6, 0.6)
    image_gain = jax.random.uniform(key_gain, (BATCH, 1, 1, 1), jnp.float32, 0.7, 1.4)
    values = field + mixes * common
    return (image_gain * height_ramp() * scales * values).astype(jnp.bfloat16)


def draw_cotangent(key, part):
    field, common = base_fields(key)
    own_key = jax.random.fold_in(key, 37)
    key_noise, key_perm, key_coef = jax.random.split(own_key, 3)
    noise = jnp.clip(jax.random.normal(key_noise, (BATCH, C, HEIGHT, IW), jnp.float32), -3.0, 3.0)
    order = jax.random.permutation(key_perm, C)
    coupled = jnp.take(field, order, axis=1)
    coupling = jax.random.uniform(key_coef, (1, C, 1, 1), jnp.float32, -0.9, 0.9)
    return (steep_ramp() * (noise + coupling * coupled)).astype(jnp.bfloat16)


def bell_draw(key, shape, width, reach, kind=jnp.bfloat16):
    array = jax.random.normal(key, shape, jnp.float32) * width
    return jnp.minimum(jnp.maximum(array, -reach), reach).astype(kind)


def setup_inputs(seed: int = 0) -> dict:
    key_of = jax.random.split(jax.random.key(seed), 5)
    return {
        "images": draw_images(jax.random.fold_in(key_of[4], 71), 0),
        "conv_w": bell_draw(key_of[1], (PATCH, C), (9 * C) ** -0.5, 0.25, jnp.float32),
        "bias": bell_draw(key_of[2], (C,), 1.0, 4.0, jnp.float32),
        "cotangent": draw_cotangent(jax.random.fold_in(key_of[4], 71), 0),
    }


eps_value = 1e-05

def tap_stack(row_slab, img_width, flipped):
    pieces = []
    for tap_row in range(3):
        for tap_col in range(3):
            first_row = 2 - tap_row if flipped else tap_row
            first_col = 2 - tap_col if flipped else tap_col
            pieces.append(row_slab[:, first_row, first_col:first_col + img_width])
    return jnp.concatenate(pieces, axis=0)

def reference(images, conv_w, bias, cotangent):
    highest = lax.Precision.HIGHEST
    pixels = BATCH * HEIGHT * IW
    patch_dim = 9 * C
    framed = jnp.pad(images, ((0, 0), (0, 0), (1, 1), (1, 1)))
    gframed = jnp.pad(cotangent, ((0, 0), (0, 0), (1, 1), (1, 1)))
    zero_index = jnp.zeros((), jnp.int32)

    def slab_of(source, row_index, count):
        image_index = (row_index // HEIGHT).astype(jnp.int32)
        row_pos = (row_index % HEIGHT).astype(jnp.int32)
        return lax.dynamic_slice(source, (image_index, zero_index, row_pos, zero_index), (1, C, count, source.shape[3]))[0]

    def moment_step(loop_state, row_index):
        gram_part, patch_sums, cross_part, grad_total = loop_state
        patches = tap_stack(slab_of(framed, row_index, 3), IW, False).astype(jnp.float32)
        grad_row = slab_of(cotangent, row_index, 1)[:, 0, :].astype(jnp.float32)
        gram_part = gram_part + jnp.dot(patches, patches.T, precision=highest)
        patch_sums = patch_sums + lax.optimization_barrier(jnp.sum(patches, axis=1))
        cross_part = cross_part + jnp.dot(patches, grad_row.T, precision=highest)
        grad_total = grad_total + lax.optimization_barrier(jnp.sum(grad_row, axis=1))
        return ((gram_part, patch_sums, cross_part, grad_total), None)
    indices = jnp.arange(BATCH * HEIGHT, dtype=jnp.int32)
    start_state = (jnp.zeros((patch_dim, patch_dim), jnp.float32), jnp.zeros((patch_dim,), jnp.float32), jnp.zeros((patch_dim, C), jnp.float32), jnp.zeros((C,), jnp.float32))
    (gram_part, patch_sums, cross_part, grad_total), _ = lax.scan(moment_step, start_state, indices)
    mean_vec = patch_sums / pixels
    identity = jnp.eye(patch_dim, dtype=jnp.float32)
    covariance = gram_part / pixels - jnp.outer(mean_vec, mean_vec) + eps_value * identity
    frob_norm = jnp.sqrt(jnp.sum(covariance * covariance))
    iter_y = covariance / frob_norm
    iter_z = identity
    for sweep in range(ITERS):
        factor = 0.5 * (3.0 * identity - jnp.dot(iter_z, iter_y, precision=highest))
        iter_y = jnp.dot(factor, iter_y, precision=highest)
        iter_z = jnp.dot(factor, iter_z, precision=highest)
    inv_root = iter_z / jnp.sqrt(frob_norm)
    mixing = jnp.dot(inv_root, conv_w, precision=highest)
    mixing_b = mixing.astype(jnp.bfloat16)
    bias_shift = bias - jnp.dot(mean_vec, mixing, precision=highest)
    grad_w = jnp.dot(inv_root.T, cross_part - jnp.outer(mean_vec, grad_total), precision=highest) / pixels
    forward_w = mixing_b.astype(jnp.float32)
    back_w = forward_w.reshape(9, C, C).transpose(1, 0, 2).reshape(C, patch_dim)

    def output_step(loop_state, row_index):
        patches = tap_stack(slab_of(framed, row_index, 3), IW, False).astype(jnp.float32)
        out_row = (jnp.dot(forward_w.T, patches, precision=highest) + bias_shift[:, None]).astype(jnp.bfloat16)
        gpatches = tap_stack(slab_of(gframed, row_index, 3), IW, True).astype(jnp.float32)
        back_row = jnp.dot(back_w, gpatches, precision=highest).astype(jnp.bfloat16)
        return (loop_state, (out_row, back_row))
    _, (out_rows, back_rows) = lax.scan(output_step, jnp.zeros((), jnp.float32), indices)
    outputs = out_rows.reshape(BATCH, HEIGHT, C, IW).transpose(0, 2, 1, 3)
    grad_x = back_rows.reshape(BATCH, HEIGHT, C, IW).transpose(0, 2, 1, 3)
    return (outputs, grad_x, grad_w)
```

```python
import jax
import jax.numpy as jnp
from jax import lax
from jax.sharding import PartitionSpec as P

ITERS = 5


eps_value = 1e-05


def with_halo(block, sides, width):
    for axis, dim in sides:
        count = lax.axis_size(axis)
        forward = [(i, i + 1) for i in range(count - 1)]
        backward = [(target, source) for source, target in forward]
        low = lax.ppermute(
            lax.slice_in_dim(block, block.shape[dim] - width, None, axis=dim), axis, forward
        )
        high = lax.ppermute(lax.slice_in_dim(block, 0, width, axis=dim), axis, backward)
        block = jnp.concatenate([low, block, high], axis=dim)
    return block


def tap_matrix(padded, strip_rows, img_width, flipped):
    channels = padded.shape[0]
    pieces = []
    for tap_row in range(3):
        for tap_col in range(3):
            first_row = 2 - tap_row if flipped else tap_row
            first_col = 2 - tap_col if flipped else tap_col
            piece = padded[:, first_row : first_row + strip_rows, first_col : first_col + img_width]
            pieces.append(piece.reshape(channels, strip_rows * img_width))
    return jnp.concatenate(pieces, axis=0)


def tree_psum(block, steps):
    trail = []
    for axis, size in steps:
        distance = 1
        while distance < size:
            half = block.shape[0] // 2
            bit = (lax.axis_index(axis) // distance) % 2
            pairs = [(i, i ^ distance) for i in range(size)]
            keep = lax.dynamic_slice_in_dim(block, bit * half, half, 0)
            send = lax.dynamic_slice_in_dim(block, (1 - bit) * half, half, 0)
            block = keep + lax.ppermute(send, axis, pairs)
            trail.append((axis, pairs, bit, half))
            distance *= 2
    for axis, pairs, bit, half in reversed(trail):
        other = lax.ppermute(block, axis, pairs)
        whole = jnp.zeros((2 * half,) + block.shape[1:], block.dtype)
        whole = lax.dynamic_update_slice_in_dim(whole, block, bit * half, 0)
        block = lax.dynamic_update_slice_in_dim(whole, other, (1 - bit) * half, 0)
    return block


def on_device(images, conv_w, bias, cotangent):
    highest = lax.Precision.HIGHEST
    channels = images.shape[1]
    strip_rows = images.shape[2]
    img_width = images.shape[3]
    patch_dim = 9 * channels
    pixels = images.shape[0] * strip_rows * img_width * lax.axis_size("rows") * lax.axis_size("dp")
    framed = with_halo(images, (("rows", 2),), 1)
    gframed = with_halo(cotangent, (("rows", 2),), 1)
    padded = jnp.pad(framed[0], ((0, 0), (0, 0), (1, 1)))
    gpadded = jnp.pad(gframed[0], ((0, 0), (0, 0), (1, 1)))
    grad_field = cotangent[0].reshape(channels, strip_rows * img_width)
    contract_last = (((1,), (1,)), ((), ()))

    stacked = jnp.concatenate(
        [tap_matrix(padded, strip_rows, img_width, False), grad_field], axis=0
    )
    moments = lax.dot_general(stacked, stacked, contract_last, preferred_element_type=jnp.float32)
    sums = jnp.sum(stacked, axis=1, dtype=jnp.float32)
    local = jnp.concatenate([moments, sums[:, None]], axis=1)
    total = tree_psum(local, (("rows", lax.axis_size("rows")), ("dp", lax.axis_size("dp"))))

    gram_whole = total[:patch_dim, :patch_dim]
    cross_total = total[:patch_dim, patch_dim : patch_dim + channels]
    patch_sums = total[:patch_dim, -1]
    grad_sum = total[patch_dim:, -1]

    mean_vec = patch_sums / pixels
    identity = jnp.eye(patch_dim, dtype=jnp.float32)
    covariance = gram_whole / pixels - jnp.outer(mean_vec, mean_vec) + eps_value * identity
    frob_norm = jnp.sqrt(jnp.sum(covariance * covariance))
    iter_y = covariance / frob_norm
    factor = 0.5 * (3.0 * identity - iter_y)
    iter_y = jnp.dot(factor, iter_y, precision=highest)
    iter_z = factor
    for sweep in range(1, ITERS):
        factor = 0.5 * (3.0 * identity - jnp.dot(iter_z, iter_y, precision=highest))
        if sweep < ITERS - 1:
            iter_y = jnp.dot(factor, iter_y, precision=highest)
        iter_z = jnp.dot(factor, iter_z, precision=highest)
    inv_root = iter_z / jnp.sqrt(frob_norm)
    mixing = jnp.dot(inv_root, conv_w, precision=highest)
    mixing_b = mixing.astype(jnp.bfloat16)
    bias_shift = bias - jnp.dot(mean_vec, mixing, precision=highest)
    grad_w = (
        jnp.dot(inv_root.T, cross_total - jnp.outer(mean_vec, grad_sum), precision=highest)
        / pixels
    )
    back_w = mixing_b.reshape(9, channels, channels).transpose(1, 0, 2).reshape(channels, patch_dim)
    contract_first = (((0,), (0,)), ((), ()))

    out_rows = lax.dot_general(
        mixing_b, stacked[:patch_dim], contract_first, preferred_element_type=jnp.float32
    )
    out_rows = (out_rows + bias_shift[:, None]).astype(jnp.bfloat16)
    gpatches = tap_matrix(gpadded, strip_rows, img_width, True)
    back_rows = jnp.dot(back_w, gpatches, preferred_element_type=jnp.float32).astype(jnp.bfloat16)
    out_buffer = out_rows.reshape(channels, strip_rows, img_width)
    back_buffer = back_rows.reshape(channels, strip_rows, img_width)
    return (out_buffer[None], back_buffer[None], grad_w)


def solution(mesh):
    placed = (P("dp", None, "rows", None), P(), P(), P("dp", None, "rows", None))
    return jax.shard_map(
        on_device,
        mesh=mesh,
        in_specs=placed,
        out_specs=(P("dp", None, "rows", None), P("dp", None, "rows", None), P()),
        check_vma=False,
    )
```

```python
import jax
import jax.numpy as jnp
from jax import lax
from jax.sharding import PartitionSpec as P

ITERS = 5


eps_value = 1e-05


def with_halo(block, sides, width):
    for axis, dim in sides:
        count = lax.axis_size(axis)
        forward = [(i, i + 1) for i in range(count - 1)]
        backward = [(target, source) for source, target in forward]
        low = lax.ppermute(
            lax.slice_in_dim(block, block.shape[dim] - width, None, axis=dim), axis, forward
        )
        high = lax.ppermute(lax.slice_in_dim(block, 0, width, axis=dim), axis, backward)
        block = jnp.concatenate([low, block, high], axis=dim)
    return block


def tap_matrix(padded, strip_rows, img_width):
    pieces = []
    for tap_row in range(3):
        for tap_col in range(3):
            pieces.append(
                padded[:, tap_row : tap_row + strip_rows, tap_col : tap_col + img_width]
            )
    return jnp.concatenate(pieces, axis=0)


def radices_of(size):
    if size % 2 == 0 and size > 2 and (size // 2) & (size // 2 - 1) == 0 and (size // 2).bit_length() % 2 == 1:
        levels, rest = [2], size // 2
    else:
        levels, rest = [], size
    while rest % 4 == 0:
        levels.append(4)
        rest //= 4
    while rest % 2 == 0:
        levels.append(2)
        rest //= 2
    assert rest == 1
    return levels


def tree_psum(block, axes):
    trail = []
    for axis in axes:
        size = lax.axis_size(axis)
        stride = 1
        for radix in radices_of(size):
            digit = (lax.axis_index(axis) // stride) % radix
            parts = block.reshape((radix, block.shape[0] // radix) + block.shape[1:])
            block = lax.dynamic_index_in_dim(parts, digit, 0, keepdims=False)
            shifts = []
            for shift in range(1, radix):
                pairs = [
                    (i, i + ((((i // stride) % radix) + shift) % radix - (i // stride) % radix) * stride)
                    for i in range(size)
                ]
                send = lax.dynamic_index_in_dim(parts, (digit + shift) % radix, 0, keepdims=False)
                block = block + lax.ppermute(send, axis, pairs)
                shifts.append(pairs)
            trail.append((axis, radix, digit, shifts))
            stride *= radix
    for axis, radix, digit, shifts in reversed(trail):
        pieces = [block] + [lax.ppermute(block, axis, pairs) for pairs in shifts]
        placed = []
        for position in range(radix):
            source = (digit - position) % radix
            value = pieces[0]
            for shift in range(1, radix):
                value = jnp.where(source == shift, pieces[shift], value)
            placed.append(value)
        block = jnp.concatenate(placed, axis=0)
    return block


def on_device(images, conv_w, bias, cotangent):
    highest = lax.Precision.HIGHEST
    channels = images.shape[1]
    strip_rows = images.shape[2]
    img_width = images.shape[3]
    patch_dim = 9 * channels
    pixels = images.shape[0] * strip_rows * img_width * lax.axis_size("rows") * lax.axis_size("dp")
    framed = with_halo(images, (("rows", 2),), 1)
    gframed = with_halo(cotangent, (("rows", 2),), 1)
    padded = jnp.pad(framed[0], ((0, 0), (0, 0), (1, 1)))
    gpadded = jnp.pad(gframed[0], ((0, 0), (0, 0), (1, 1)))
    contract_pixels = (((1, 2), (1, 2)), ((), ()))

    stacked = jnp.concatenate([tap_matrix(padded, strip_rows, img_width), cotangent[0]], axis=0)
    moments = lax.dot_general(
        stacked, stacked, contract_pixels, preferred_element_type=jnp.float32
    )
    sums = jnp.sum(stacked, axis=(1, 2), dtype=jnp.float32)
    local = jnp.concatenate([moments, sums[:, None]], axis=1)
    total = tree_psum(local, ("rows", "dp"))

    gram_whole = total[:patch_dim, :patch_dim]
    cross_total = total[:patch_dim, patch_dim : patch_dim + channels]
    patch_sums = total[:patch_dim, -1]
    grad_sum = total[patch_dim:, -1]

    mean_vec = patch_sums / pixels
    identity = jnp.eye(patch_dim, dtype=jnp.float32)
    covariance = gram_whole / pixels - jnp.outer(mean_vec, mean_vec) + eps_value * identity
    frob_norm = jnp.sqrt(jnp.sum(covariance * covariance))
    iter_y = covariance / frob_norm
    factor = 0.5 * (3.0 * identity - iter_y)
    iter_y = jnp.dot(factor, iter_y, precision=highest)
    iter_z = factor
    for sweep in range(1, ITERS):
        factor = 0.5 * (3.0 * identity - jnp.dot(iter_z, iter_y, precision=highest))
        if sweep < ITERS - 1:
            iter_y = jnp.dot(factor, iter_y, precision=highest)
        iter_z = jnp.dot(factor, iter_z, precision=highest)
    inv_root = iter_z / jnp.sqrt(frob_norm)
    mixing = jnp.dot(inv_root, conv_w, precision=highest)
    mixing_b = mixing.astype(jnp.bfloat16)
    bias_shift = bias - jnp.dot(mean_vec, mixing, precision=highest)
    grad_w = (
        jnp.dot(inv_root.T, cross_total - jnp.outer(mean_vec, grad_sum), precision=highest)
        / pixels
    )
    contract_first = (((0,), (0,)), ((), ()))
    out_rows = lax.dot_general(
        mixing_b, stacked[:patch_dim], contract_first, preferred_element_type=jnp.float32
    )
    out_buffer = (out_rows + bias_shift[:, None, None]).astype(jnp.bfloat16)
    back_kernel = mixing_b.reshape(3, 3, channels, channels)[::-1, ::-1]
    back_rows = lax.conv_general_dilated(
        gpadded[None],
        back_kernel,
        window_strides=(1, 1),
        padding="VALID",
        dimension_numbers=("NCHW", "HWOI", "NCHW"),
        preferred_element_type=jnp.float32,
    )
    back_buffer = back_rows.astype(jnp.bfloat16)
    return (out_buffer[None], back_buffer, grad_w)


def solution(mesh):
    placed = (P("dp", None, "rows", None), P(), P(), P("dp", None, "rows", None))
    return jax.shard_map(
        on_device,
        mesh=mesh,
        in_specs=placed,
        out_specs=(P("dp", None, "rows", None), P("dp", None, "rows", None), P()),
        check_vma=False,
    )
```

```python
import jax
import jax.numpy as jnp
from jax import lax
from jax.sharding import PartitionSpec as P

ITERS = 5


eps_value = 1e-05


def with_halo(block, sides, width):
    for axis, dim in sides:
        count = lax.axis_size(axis)
        forward = [(i, i + 1) for i in range(count - 1)]
        backward = [(target, source) for source, target in forward]
        low = lax.ppermute(
            lax.slice_in_dim(block, block.shape[dim] - width, None, axis=dim), axis, forward
        )
        high = lax.ppermute(lax.slice_in_dim(block, 0, width, axis=dim), axis, backward)
        block = jnp.concatenate([low, block, high], axis=dim)
    return block


def tap_stack(padded, strip_rows, img_width, flipped):
    shifted = [padded[:, :, first_col : first_col + img_width] for first_col in range(3)]
    pieces = []
    for tap_row in range(3):
        for tap_col in range(3):
            first_row = 2 - tap_row if flipped else tap_row
            first_col = 2 - tap_col if flipped else tap_col
            pieces.append(shifted[first_col][first_row : first_row + strip_rows])
    return pieces


def tree_psum(block, axes, levels):
    size = 1
    for axis in axes:
        size *= lax.axis_size(axis)
    index = 0
    for axis in axes:
        index = index * lax.axis_size(axis) + lax.axis_index(axis)
    trail = []
    for stride, radix in levels:
        digit = (index // stride) % radix
        parts = block.reshape((radix, block.shape[0] // radix) + block.shape[1:])
        block = lax.dynamic_index_in_dim(parts, digit, 0, keepdims=False)
        shifts = []
        for shift in range(1, radix):
            pairs = [
                (i, i + ((((i // stride) % radix) + shift) % radix - (i // stride) % radix) * stride)
                for i in range(size)
            ]
            send = lax.dynamic_index_in_dim(parts, (digit + shift) % radix, 0, keepdims=False)
            block = block + lax.ppermute(send, axes, pairs)
            shifts.append(pairs)
        trail.append((radix, digit, shifts))
    for radix, digit, shifts in reversed(trail):
        pieces = [block] + [lax.ppermute(block, axes, pairs) for pairs in shifts]
        placed = []
        for position in range(radix):
            source = (digit - position) % radix
            value = pieces[0]
            for shift in range(1, radix):
                value = jnp.where(source == shift, pieces[shift], value)
            placed.append(value)
        block = jnp.concatenate(placed, axis=0)
    return block


def physical_levels(mesh_sizes):
    levels, stride, rest = [], 1, mesh_sizes
    if rest % 2 == 0 and rest > 2 and ((rest // 2) & (rest // 2 - 1)) == 0 and (rest // 2).bit_length() % 2 == 1:
        levels.append((1, 2))
        stride, rest = 2, rest // 2
    while rest % 4 == 0:
        levels.append((stride, 4))
        stride, rest = stride * 4, rest // 4
    while rest % 2 == 0:
        levels.append((stride, 2))
        stride, rest = stride * 2, rest // 2
    return levels


def on_device(images, conv_w, bias, cotangent):
    highest = lax.Precision.HIGHEST
    channels = images.shape[1]
    strip_rows = images.shape[2]
    img_width = images.shape[3]
    patch_dim = 9 * channels
    pixels = images.shape[0] * strip_rows * img_width * lax.axis_size("rows") * lax.axis_size("dp")
    rows_first = images[0].transpose(1, 0, 2)
    grad_first = cotangent[0].transpose(1, 0, 2)
    framed = with_halo(rows_first, (("rows", 0),), 1)
    gframed = with_halo(grad_first, (("rows", 0),), 1)
    padded = jnp.pad(framed, ((0, 0), (0, 0), (1, 1)))
    gpadded = jnp.pad(gframed, ((0, 0), (0, 0), (1, 1)))
    contract_pixels = (((0, 2), (0, 2)), ((), ()))

    stacked = jnp.concatenate(tap_stack(padded, strip_rows, img_width, False) + [grad_first], axis=1)
    moments = lax.dot_general(
        stacked, stacked, contract_pixels, preferred_element_type=jnp.float32
    )
    sums = jnp.sum(stacked, axis=(0, 2), dtype=jnp.float32)
    local = jnp.concatenate([moments, sums[:, None]], axis=1)
    world = lax.axis_size("dp") * lax.axis_size("rows")
    total = tree_psum(local, ("dp", "rows"), physical_levels(world))

    gram_whole = total[:patch_dim, :patch_dim]
    cross_total = total[:patch_dim, patch_dim : patch_dim + channels]
    patch_sums = total[:patch_dim, -1]
    grad_sum = total[patch_dim:, -1]

    mean_vec = patch_sums / pixels
    identity = jnp.eye(patch_dim, dtype=jnp.float32)
    covariance = gram_whole / pixels - jnp.outer(mean_vec, mean_vec) + eps_value * identity
    frob_norm = jnp.sqrt(jnp.sum(covariance * covariance))
    iter_y = covariance / frob_norm
    factor = 0.5 * (3.0 * identity - iter_y)
    iter_y = jnp.dot(factor, iter_y, precision=highest)
    iter_z = factor
    for sweep in range(1, ITERS):
        factor = 0.5 * (3.0 * identity - jnp.dot(iter_z, iter_y, precision=highest))
        if sweep < ITERS - 1:
            iter_y = jnp.dot(factor, iter_y, precision=highest)
        iter_z = jnp.dot(factor, iter_z, precision=highest)
    inv_root = iter_z / jnp.sqrt(frob_norm)
    mixing = jnp.dot(inv_root, conv_w, precision=highest)
    mixing_b = mixing.astype(jnp.bfloat16)
    bias_shift = bias - jnp.dot(mean_vec, mixing, precision=highest)
    grad_w = (
        jnp.dot(inv_root.T, cross_total - jnp.outer(mean_vec, grad_sum), precision=highest)
        / pixels
    )
    back_w = mixing_b.reshape(9, channels, channels).transpose(1, 0, 2).reshape(channels, patch_dim)
    contract_taps = (((0,), (1,)), ((), ()))
    out_rows = lax.dot_general(
        mixing_b, stacked[:, :patch_dim], contract_taps, preferred_element_type=jnp.float32
    )
    out_buffer = (out_rows + bias_shift[:, None, None]).astype(jnp.bfloat16)
    gstacked = jnp.concatenate(tap_stack(gpadded, strip_rows, img_width, True), axis=1)
    contract_back = (((1,), (1,)), ((), ()))
    back_rows = lax.dot_general(
        back_w, gstacked, contract_back, preferred_element_type=jnp.float32
    )
    back_buffer = back_rows.astype(jnp.bfloat16)
    return (out_buffer[None], back_buffer[None], grad_w)


def solution(mesh):
    placed = (P("dp", None, "rows", None), P(), P(), P("dp", None, "rows", None))
    return jax.shard_map(
        on_device,
        mesh=mesh,
        in_specs=placed,
        out_specs=(P("dp", None, "rows", None), P("dp", None, "rows", None), P()),
        check_vma=False,
    )
```

```python
import jax
import jax.numpy as jnp
from jax import lax
from jax.sharding import PartitionSpec as P

ITERS = 5


eps_value = 1e-05


def with_halo(block, sides, width):
    for axis, dim in sides:
        count = lax.axis_size(axis)
        forward = [(i, i + 1) for i in range(count - 1)]
        backward = [(target, source) for source, target in forward]
        low = lax.ppermute(
            lax.slice_in_dim(block, block.shape[dim] - width, None, axis=dim), axis, forward
        )
        high = lax.ppermute(lax.slice_in_dim(block, 0, width, axis=dim), axis, backward)
        block = jnp.concatenate([low, block, high], axis=dim)
    return block


def column_taps(padded, img_width, flipped):
    order = (2, 1, 0) if flipped else (0, 1, 2)
    return jnp.concatenate([padded[:, :, first : first + img_width] for first in order], axis=1)


def tree_psum(block, axes, levels):
    size = 1
    for axis in axes:
        size *= lax.axis_size(axis)
    index = 0
    for axis in axes:
        index = index * lax.axis_size(axis) + lax.axis_index(axis)
    trail = []
    for stride, radix in levels:
        digit = (index // stride) % radix
        parts = block.reshape((radix, block.shape[0] // radix) + block.shape[1:])
        block = lax.dynamic_index_in_dim(parts, digit, 0, keepdims=False)
        shifts = []
        for shift in range(1, radix):
            pairs = [
                (i, i + ((((i // stride) % radix) + shift) % radix - (i // stride) % radix) * stride)
                for i in range(size)
            ]
            send = lax.dynamic_index_in_dim(parts, (digit + shift) % radix, 0, keepdims=False)
            block = block + lax.ppermute(send, axes, pairs)
            shifts.append(pairs)
        trail.append((radix, digit, shifts))
    for radix, digit, shifts in reversed(trail):
        pieces = [block] + [lax.ppermute(block, axes, pairs) for pairs in shifts]
        placed = []
        for position in range(radix):
            source = (digit - position) % radix
            value = pieces[0]
            for shift in range(1, radix):
                value = jnp.where(source == shift, pieces[shift], value)
            placed.append(value)
        block = jnp.concatenate(placed, axis=0)
    return block


def physical_levels(mesh_sizes):
    levels, stride, rest = [], 1, mesh_sizes
    if rest % 2 == 0 and rest > 2 and ((rest // 2) & (rest // 2 - 1)) == 0 and (rest // 2).bit_length() % 2 == 1:
        levels.append((1, 2))
        stride, rest = 2, rest // 2
    while rest % 4 == 0:
        levels.append((stride, 4))
        stride, rest = stride * 4, rest // 4
    while rest % 2 == 0:
        levels.append((stride, 2))
        stride, rest = stride * 2, rest // 2
    return levels


def on_device(images, conv_w, bias, cotangent):
    highest = lax.Precision.HIGHEST
    channels = images.shape[1]
    strip_rows = images.shape[2]
    img_width = images.shape[3]
    patch_dim = 9 * channels
    pixels = images.shape[0] * strip_rows * img_width * lax.axis_size("rows") * lax.axis_size("dp")
    rows_first = images[0].transpose(1, 0, 2)
    grad_first = cotangent[0].transpose(1, 0, 2)
    framed = with_halo(rows_first, (("rows", 0),), 1)
    gframed = with_halo(grad_first, (("rows", 0),), 1)
    padded = jnp.pad(framed, ((0, 0), (0, 0), (1, 1)))
    gpadded = jnp.pad(gframed, ((0, 0), (0, 0), (1, 1)))
    contract_pixels = (((0, 2), (0, 2)), ((), ()))

    taps = column_taps(padded, img_width, False)
    band = 3 * channels

    def block_of(first, second):
        return lax.dot_general(
            taps[first : first + strip_rows],
            taps[second : second + strip_rows],
            contract_pixels,
            preferred_element_type=jnp.float32,
        )

    upper = {(i, j): block_of(i, j) for i in range(3) for j in range(i, 3)}
    gram_rows = [
        jnp.concatenate([upper[(i, j)] if j >= i else upper[(j, i)].T for j in range(3)], axis=1)
        for i in range(3)
    ]
    gram_part = jnp.concatenate(gram_rows, axis=0)
    cross_part = jnp.concatenate(
        [
            lax.dot_general(
                taps[i : i + strip_rows], grad_first, contract_pixels, preferred_element_type=jnp.float32
            )
            for i in range(3)
        ],
        axis=0,
    )
    row_sums = jnp.sum(taps, axis=2, dtype=jnp.float32)
    patch_part = jnp.concatenate([jnp.sum(row_sums[i : i + strip_rows], axis=0) for i in range(3)])
    grad_part = jnp.sum(grad_first, axis=(0, 2), dtype=jnp.float32)
    top = jnp.concatenate([gram_part, cross_part, patch_part[:, None]], axis=1)
    bottom = jnp.concatenate(
        [jnp.zeros((channels, patch_dim + channels), jnp.float32), grad_part[:, None]], axis=1
    )
    local = jnp.concatenate([top, bottom], axis=0)
    world = lax.axis_size("dp") * lax.axis_size("rows")
    total = tree_psum(local, ("dp", "rows"), physical_levels(world))

    gram_whole = total[:patch_dim, :patch_dim]
    cross_total = total[:patch_dim, patch_dim : patch_dim + channels]
    patch_sums = total[:patch_dim, -1]
    grad_sum = total[patch_dim:, -1]

    mean_vec = patch_sums / pixels
    identity = jnp.eye(patch_dim, dtype=jnp.float32)
    covariance = gram_whole / pixels - jnp.outer(mean_vec, mean_vec) + eps_value * identity
    frob_norm = jnp.sqrt(jnp.sum(covariance * covariance))
    iter_y = covariance / frob_norm
    factor = 0.5 * (3.0 * identity - iter_y)
    iter_y = jnp.dot(factor, iter_y, precision=highest)
    iter_z = factor
    for sweep in range(1, ITERS):
        factor = 0.5 * (3.0 * identity - jnp.dot(iter_z, iter_y, precision=highest))
        if sweep < ITERS - 1:
            iter_y = jnp.dot(factor, iter_y, precision=highest)
        iter_z = jnp.dot(factor, iter_z, precision=highest)
    inv_root = iter_z / jnp.sqrt(frob_norm)
    mixing = jnp.dot(inv_root, conv_w, precision=highest)
    mixing_b = mixing.astype(jnp.bfloat16)
    bias_shift = bias - jnp.dot(mean_vec, mixing, precision=highest)
    grad_w = (
        jnp.dot(inv_root.T, cross_total - jnp.outer(mean_vec, grad_sum), precision=highest)
        / pixels
    )
    contract_band = (((0,), (1,)), ((), ()))
    forward_bands = mixing_b.reshape(3, band, channels)
    out_rows = bias_shift[:, None, None]
    for i in range(3):
        out_rows = out_rows + lax.dot_general(
            forward_bands[i], taps[i : i + strip_rows], contract_band, preferred_element_type=jnp.float32
        )
    out_buffer = out_rows.astype(jnp.bfloat16)
    gtaps = column_taps(gpadded, img_width, True)
    flipped = mixing_b.reshape(3, 3, channels, channels)[::-1]
    back_bands = flipped.transpose(0, 2, 1, 3).reshape(3, channels, band)
    contract_back = (((1,), (1,)), ((), ()))
    back_rows = None
    for i in range(3):
        term = lax.dot_general(
            back_bands[i], gtaps[i : i + strip_rows], contract_back, preferred_element_type=jnp.float32
        )
        back_rows = term if back_rows is None else back_rows + term
    back_buffer = back_rows.astype(jnp.bfloat16)
    return (out_buffer[None], back_buffer[None], grad_w)


def solution(mesh):
    placed = (P("dp", None, "rows", None), P(), P(), P("dp", None, "rows", None))
    return jax.shard_map(
        on_device,
        mesh=mesh,
        in_specs=placed,
        out_specs=(P("dp", None, "rows", None), P("dp", None, "rows", None), P()),
        check_vma=False,
    )
```

```python
import jax
import jax.numpy as jnp
from jax import lax
from jax.sharding import PartitionSpec as P

ITERS = 5


eps_value = 1e-05


def with_halo(block, sides, width):
    for axis, dim in sides:
        count = lax.axis_size(axis)
        forward = [(i, i + 1) for i in range(count - 1)]
        backward = [(target, source) for source, target in forward]
        low = lax.ppermute(
            lax.slice_in_dim(block, block.shape[dim] - width, None, axis=dim), axis, forward
        )
        high = lax.ppermute(lax.slice_in_dim(block, 0, width, axis=dim), axis, backward)
        block = jnp.concatenate([low, block, high], axis=dim)
    return block


def column_taps(padded, img_width, flipped):
    order = (2, 1, 0) if flipped else (0, 1, 2)
    return jnp.concatenate([padded[:, :, first : first + img_width] for first in order], axis=1)


def tree_psum(block, axes, levels):
    size = 1
    for axis in axes:
        size *= lax.axis_size(axis)
    index = 0
    for axis in axes:
        index = index * lax.axis_size(axis) + lax.axis_index(axis)
    trail = []
    for stride, radix in levels:
        digit = (index // stride) % radix
        parts = block.reshape((radix, block.shape[0] // radix) + block.shape[1:])
        block = lax.dynamic_index_in_dim(parts, digit, 0, keepdims=False)
        shifts = []
        for shift in range(1, radix):
            pairs = [
                (i, i + ((((i // stride) % radix) + shift) % radix - (i // stride) % radix) * stride)
                for i in range(size)
            ]
            send = lax.dynamic_index_in_dim(parts, (digit + shift) % radix, 0, keepdims=False)
            block = block + lax.ppermute(send, axes, pairs)
            shifts.append(pairs)
        trail.append((radix, digit, shifts))
    for radix, digit, shifts in reversed(trail):
        pieces = [block] + [lax.ppermute(block, axes, pairs) for pairs in shifts]
        placed = []
        for position in range(radix):
            source = (digit - position) % radix
            value = pieces[0]
            for shift in range(1, radix):
                value = jnp.where(source == shift, pieces[shift], value)
            placed.append(value)
        block = jnp.concatenate(placed, axis=0)
    return block


def physical_levels(mesh_sizes):
    levels, stride, rest = [], 1, mesh_sizes
    if rest % 2 == 0 and rest > 2 and ((rest // 2) & (rest // 2 - 1)) == 0 and (rest // 2).bit_length() % 2 == 1:
        levels.append((1, 2))
        stride, rest = 2, rest // 2
    while rest % 4 == 0:
        levels.append((stride, 4))
        stride, rest = stride * 4, rest // 4
    while rest % 2 == 0:
        levels.append((stride, 2))
        stride, rest = stride * 2, rest // 2
    return levels


def on_device(images, conv_w, bias, cotangent):
    highest = lax.Precision.HIGHEST
    channels = images.shape[1]
    strip_rows = images.shape[2]
    img_width = images.shape[3]
    patch_dim = 9 * channels
    pixels = images.shape[0] * strip_rows * img_width * lax.axis_size("rows") * lax.axis_size("dp")
    rows_first = images[0].transpose(1, 0, 2)
    grad_first = cotangent[0].transpose(1, 0, 2)
    framed = with_halo(rows_first, (("rows", 0),), 1)
    gframed = with_halo(grad_first, (("rows", 0),), 1)
    padded = jnp.pad(framed, ((0, 0), (0, 0), (1, 1)))
    gpadded = jnp.pad(gframed, ((0, 0), (0, 0), (1, 1)))
    contract_pixels = (((0, 2), (0, 2)), ((), ()))

    taps = column_taps(padded, img_width, False)
    band = 3 * channels

    def block_of(first, second):
        return lax.dot_general(
            taps[first : first + strip_rows],
            taps[second : second + strip_rows],
            contract_pixels,
            preferred_element_type=jnp.float32,
        )

    upper = {(i, j): block_of(i, j) for i in range(3) for j in range(i, 3)}
    gram_rows = [
        jnp.concatenate([upper[(i, j)] if j >= i else upper[(j, i)].T for j in range(3)], axis=1)
        for i in range(3)
    ]
    gram_part = jnp.concatenate(gram_rows, axis=0)
    cross_part = jnp.concatenate(
        [
            lax.dot_general(
                taps[i : i + strip_rows], grad_first, contract_pixels, preferred_element_type=jnp.float32
            )
            for i in range(3)
        ],
        axis=0,
    )
    row_sums = jnp.sum(taps, axis=2, dtype=jnp.float32)
    patch_part = jnp.concatenate([jnp.sum(row_sums[i : i + strip_rows], axis=0) for i in range(3)])
    grad_part = jnp.sum(grad_first, axis=(0, 2), dtype=jnp.float32)
    top = jnp.concatenate([gram_part, cross_part, patch_part[:, None]], axis=1)
    bottom = jnp.concatenate(
        [jnp.zeros((channels, patch_dim + channels), jnp.float32), grad_part[:, None]], axis=1
    )
    local = jnp.concatenate([top, bottom], axis=0)
    world = lax.axis_size("dp") * lax.axis_size("rows")
    total = tree_psum(local, ("dp", "rows"), physical_levels(world))

    gram_whole = total[:patch_dim, :patch_dim]
    cross_total = total[:patch_dim, patch_dim : patch_dim + channels]
    patch_sums = total[:patch_dim, -1]
    grad_sum = total[patch_dim:, -1]

    mean_vec = patch_sums / pixels
    identity = jnp.eye(patch_dim, dtype=jnp.float32)
    covariance = gram_whole / pixels - jnp.outer(mean_vec, mean_vec) + eps_value * identity
    frob_norm = jnp.sqrt(jnp.sum(covariance * covariance))
    iter_y = covariance / frob_norm
    factor = 0.5 * (3.0 * identity - iter_y)
    sweep_precision = lax.Precision.HIGH
    iter_y = jnp.dot(factor, iter_y, precision=sweep_precision)
    iter_z = factor
    for sweep in range(1, ITERS):
        factor = 0.5 * (3.0 * identity - jnp.dot(iter_z, iter_y, precision=sweep_precision))
        if sweep < ITERS - 1:
            iter_y = jnp.dot(factor, iter_y, precision=sweep_precision)
        iter_z = jnp.dot(factor, iter_z, precision=sweep_precision)
    inv_root = iter_z / jnp.sqrt(frob_norm)
    mixing = jnp.dot(inv_root, conv_w, precision=highest)
    mixing_b = mixing.astype(jnp.bfloat16)
    bias_shift = bias - jnp.dot(mean_vec, mixing, precision=highest)
    grad_w = (
        jnp.dot(inv_root.T, cross_total - jnp.outer(mean_vec, grad_sum), precision=highest)
        / pixels
    )
    contract_band = (((0,), (1,)), ((), ()))
    forward_bands = mixing_b.reshape(3, band, channels)
    out_rows = bias_shift[:, None, None]
    for i in range(3):
        out_rows = out_rows + lax.dot_general(
            forward_bands[i], taps[i : i + strip_rows], contract_band, preferred_element_type=jnp.float32
        )
    out_buffer = out_rows.astype(jnp.bfloat16)
    gtaps = column_taps(gpadded, img_width, True)
    flipped = mixing_b.reshape(3, 3, channels, channels)[::-1]
    back_bands = flipped.transpose(0, 2, 1, 3).reshape(3, channels, band)
    contract_back = (((1,), (1,)), ((), ()))
    back_rows = None
    for i in range(3):
        term = lax.dot_general(
            back_bands[i], gtaps[i : i + strip_rows], contract_back, preferred_element_type=jnp.float32
        )
        back_rows = term if back_rows is None else back_rows + term
    back_buffer = back_rows.astype(jnp.bfloat16)
    return (out_buffer[None], back_buffer[None], grad_w)


def solution(mesh):
    placed = (P("dp", None, "rows", None), P(), P(), P("dp", None, "rows", None))
    return jax.shard_map(
        on_device,
        mesh=mesh,
        in_specs=placed,
        out_specs=(P("dp", None, "rows", None), P("dp", None, "rows", None), P()),
        check_vma=False,
    )
```

```python
import jax
import jax.numpy as jnp
from jax import lax
from jax.sharding import PartitionSpec as P

ITERS = 5


eps_value = 1e-05


def with_halo(block, sides, width):
    for axis, dim in sides:
        count = lax.axis_size(axis)
        forward = [(i, i + 1) for i in range(count - 1)]
        backward = [(target, source) for source, target in forward]
        low = lax.ppermute(
            lax.slice_in_dim(block, block.shape[dim] - width, None, axis=dim), axis, forward
        )
        high = lax.ppermute(lax.slice_in_dim(block, 0, width, axis=dim), axis, backward)
        block = jnp.concatenate([low, block, high], axis=dim)
    return block


def column_taps(padded, img_width, flipped):
    order = (2, 1, 0) if flipped else (0, 1, 2)
    return jnp.concatenate([padded[:, :, first : first + img_width] for first in order], axis=1)


def tree_psum(block, axes, levels):
    size = 1
    for axis in axes:
        size *= lax.axis_size(axis)
    index = 0
    for axis in axes:
        index = index * lax.axis_size(axis) + lax.axis_index(axis)
    trail = []
    for stride, radix in levels:
        digit = (index // stride) % radix
        parts = block.reshape((radix, block.shape[0] // radix) + block.shape[1:])
        block = lax.dynamic_index_in_dim(parts, digit, 0, keepdims=False)
        shifts = []
        for shift in range(1, radix):
            pairs = [
                (i, i + ((((i // stride) % radix) + shift) % radix - (i // stride) % radix) * stride)
                for i in range(size)
            ]
            send = lax.dynamic_index_in_dim(parts, (digit + shift) % radix, 0, keepdims=False)
            block = block + lax.ppermute(send, axes, pairs)
            shifts.append(pairs)
        trail.append((radix, digit, shifts))
    for radix, digit, shifts in reversed(trail):
        pieces = [block] + [lax.ppermute(block, axes, pairs) for pairs in shifts]
        placed = []
        for position in range(radix):
            source = (digit - position) % radix
            value = pieces[0]
            for shift in range(1, radix):
                value = jnp.where(source == shift, pieces[shift], value)
            placed.append(value)
        block = jnp.concatenate(placed, axis=0)
    return block


def physical_levels(mesh_sizes):
    levels, stride, rest = [], 1, mesh_sizes
    if rest % 2 == 0 and rest > 2 and ((rest // 2) & (rest // 2 - 1)) == 0 and (rest // 2).bit_length() % 2 == 1:
        levels.append((1, 2))
        stride, rest = 2, rest // 2
    while rest % 4 == 0:
        levels.append((stride, 4))
        stride, rest = stride * 4, rest // 4
    while rest % 2 == 0:
        levels.append((stride, 2))
        stride, rest = stride * 2, rest // 2
    return levels


def on_device(images, conv_w, bias, cotangent):
    highest = lax.Precision.HIGHEST
    channels = images.shape[1]
    strip_rows = images.shape[2]
    img_width = images.shape[3]
    patch_dim = 9 * channels
    pixels = images.shape[0] * strip_rows * img_width * lax.axis_size("rows") * lax.axis_size("dp")
    rows_first = images[0].transpose(1, 0, 2)
    grad_first = cotangent[0].transpose(1, 0, 2)
    framed = with_halo(rows_first, (("rows", 0),), 1)
    gframed = with_halo(grad_first, (("rows", 0),), 1)
    padded = jnp.pad(framed, ((0, 0), (0, 0), (1, 1)))
    gpadded = jnp.pad(gframed, ((0, 0), (0, 0), (1, 1)))
    contract_pixels = (((0, 2), (0, 2)), ((), ()))

    taps = column_taps(padded, img_width, False)
    band = 3 * channels

    def block_of(first, second):
        return lax.dot_general(
            taps[first : first + strip_rows],
            taps[second : second + strip_rows],
            contract_pixels,
            preferred_element_type=jnp.float32,
        )

    upper = {(i, j): block_of(i, j) for i in range(3) for j in range(i, 3)}
    order = sorted(upper)
    paired = jnp.concatenate(
        [jnp.concatenate([upper[order[2 * n]], upper[order[2 * n + 1]]], axis=1) for n in range(3)], axis=0
    )
    cross_part = jnp.concatenate(
        [
            lax.dot_general(
                taps[i : i + strip_rows], grad_first, contract_pixels, preferred_element_type=jnp.float32
            )
            for i in range(3)
        ],
        axis=0,
    )
    row_sums = jnp.sum(taps, axis=2, dtype=jnp.float32)
    patch_part = jnp.concatenate([jnp.sum(row_sums[i : i + strip_rows], axis=0) for i in range(3)])
    grad_part = jnp.sum(grad_first, axis=(0, 2), dtype=jnp.float32)
    grad_column = jnp.zeros((patch_dim,), jnp.float32).at[:channels].set(grad_part)
    lanes = 128
    tail = jnp.concatenate(
        [
            cross_part,
            patch_part[:, None],
            grad_column[:, None],
            jnp.zeros((patch_dim, lanes - channels - 2), jnp.float32),
        ],
        axis=1,
    )
    top = jnp.concatenate([paired, tail], axis=1)
    world = lax.axis_size("dp") * lax.axis_size("rows")
    padded_rows = -(-patch_dim // world) * world
    local = jnp.concatenate([top, jnp.zeros((padded_rows - patch_dim, top.shape[1]), jnp.float32)], axis=0)
    total = tree_psum(local, ("dp", "rows"), physical_levels(world))

    reduced = {}
    for n in range(3):
        for m in range(2):
            reduced[order[2 * n + m]] = total[n * band : (n + 1) * band, m * band : (m + 1) * band]
    gram_whole = jnp.concatenate(
        [
            jnp.concatenate([reduced[(i, j)] if j >= i else reduced[(j, i)].T for j in range(3)], axis=1)
            for i in range(3)
        ],
        axis=0,
    )
    tail_total = total[:patch_dim, 2 * band :]
    cross_total = tail_total[:, :channels]
    patch_sums = tail_total[:, channels]
    grad_sum = tail_total[:channels, channels + 1]

    mean_vec = patch_sums / pixels
    identity = jnp.eye(patch_dim, dtype=jnp.float32)
    covariance = gram_whole / pixels - jnp.outer(mean_vec, mean_vec) + eps_value * identity
    frob_norm = jnp.sqrt(jnp.sum(covariance * covariance))
    iter_y = covariance / frob_norm
    factor = 0.5 * (3.0 * identity - iter_y)
    iter_y = jnp.dot(factor, iter_y, precision=highest)
    iter_z = factor
    for sweep in range(1, ITERS):
        factor = 0.5 * (3.0 * identity - jnp.dot(iter_z, iter_y, precision=highest))
        if sweep < ITERS - 1:
            iter_y = jnp.dot(factor, iter_y, precision=highest)
        iter_z = jnp.dot(factor, iter_z, precision=highest)
    inv_root = iter_z / jnp.sqrt(frob_norm)
    mixing = jnp.dot(inv_root, conv_w, precision=highest)
    mixing_b = mixing.astype(jnp.bfloat16)
    bias_shift = bias - jnp.dot(mean_vec, mixing, precision=highest)
    grad_w = (
        jnp.dot(inv_root.T, cross_total - jnp.outer(mean_vec, grad_sum), precision=highest)
        / pixels
    )
    contract_band = (((0,), (1,)), ((), ()))
    forward_bands = mixing_b.reshape(3, band, channels)
    out_rows = bias_shift[:, None, None]
    for i in range(3):
        out_rows = out_rows + lax.dot_general(
            forward_bands[i], taps[i : i + strip_rows], contract_band, preferred_element_type=jnp.float32
        )
    out_buffer = out_rows.astype(jnp.bfloat16)
    gtaps = column_taps(gpadded, img_width, True)
    flipped = mixing_b.reshape(3, 3, channels, channels)[::-1]
    back_bands = flipped.transpose(0, 2, 1, 3).reshape(3, channels, band)
    contract_back = (((1,), (1,)), ((), ()))
    back_rows = None
    for i in range(3):
        term = lax.dot_general(
            back_bands[i], gtaps[i : i + strip_rows], contract_back, preferred_element_type=jnp.float32
        )
        back_rows = term if back_rows is None else back_rows + term
    back_buffer = back_rows.astype(jnp.bfloat16)
    return (out_buffer[None], back_buffer[None], grad_w)


def solution(mesh):
    placed = (P("dp", None, "rows", None), P(), P(), P("dp", None, "rows", None))
    return jax.shard_map(
        on_device,
        mesh=mesh,
        in_specs=placed,
        out_specs=(P("dp", None, "rows", None), P("dp", None, "rows", None), P()),
        check_vma=False,
    )
```

```python
import jax
import jax.numpy as jnp
from jax import lax
from jax.sharding import PartitionSpec as P

ITERS = 5


eps_value = 1e-05


def with_halo(block, sides, width):
    for axis, dim in sides:
        count = lax.axis_size(axis)
        forward = [(i, i + 1) for i in range(count - 1)]
        backward = [(target, source) for source, target in forward]
        low = lax.ppermute(
            lax.slice_in_dim(block, block.shape[dim] - width, None, axis=dim), axis, forward
        )
        high = lax.ppermute(lax.slice_in_dim(block, 0, width, axis=dim), axis, backward)
        block = jnp.concatenate([low, block, high], axis=dim)
    return block


def column_taps(padded, img_width, flipped):
    order = (2, 1, 0) if flipped else (0, 1, 2)
    return jnp.concatenate([padded[:, :, first : first + img_width] for first in order], axis=1)


def tree_psum(block, axes, levels):
    size = 1
    for axis in axes:
        size *= lax.axis_size(axis)
    index = 0
    for axis in axes:
        index = index * lax.axis_size(axis) + lax.axis_index(axis)
    trail = []
    for stride, radix in levels:
        digit = (index // stride) % radix
        parts = block.reshape((radix, block.shape[0] // radix) + block.shape[1:])
        block = lax.dynamic_index_in_dim(parts, digit, 0, keepdims=False)
        shifts = []
        for shift in range(1, radix):
            pairs = [
                (i, i + ((((i // stride) % radix) + shift) % radix - (i // stride) % radix) * stride)
                for i in range(size)
            ]
            send = lax.dynamic_index_in_dim(parts, (digit + shift) % radix, 0, keepdims=False)
            block = block + lax.ppermute(send, axes, pairs)
            shifts.append(pairs)
        trail.append((radix, digit, shifts))
    for radix, digit, shifts in reversed(trail):
        pieces = [block] + [lax.ppermute(block, axes, pairs) for pairs in shifts]
        placed = []
        for position in range(radix):
            source = (digit - position) % radix
            value = pieces[0]
            for shift in range(1, radix):
                value = jnp.where(source == shift, pieces[shift], value)
            placed.append(value)
        block = jnp.concatenate(placed, axis=0)
    return block


def physical_levels(mesh_sizes):
    levels, stride, rest = [], 1, mesh_sizes
    if rest % 2 == 0 and rest > 2 and ((rest // 2) & (rest // 2 - 1)) == 0 and (rest // 2).bit_length() % 2 == 1:
        levels.append((1, 2))
        stride, rest = 2, rest // 2
    while rest % 4 == 0:
        levels.append((stride, 4))
        stride, rest = stride * 4, rest // 4
    while rest % 2 == 0:
        levels.append((stride, 2))
        stride, rest = stride * 2, rest // 2
    return levels


def on_device(images, conv_w, bias, cotangent):
    highest = lax.Precision.HIGHEST
    channels = images.shape[1]
    strip_rows = images.shape[2]
    img_width = images.shape[3]
    patch_dim = 9 * channels
    pixels = images.shape[0] * strip_rows * img_width * lax.axis_size("rows") * lax.axis_size("dp")
    rows_first = images[0].transpose(1, 0, 2)
    grad_first = cotangent[0].transpose(1, 0, 2)
    framed = with_halo(rows_first, (("rows", 0),), 1)
    gframed = with_halo(grad_first, (("rows", 0),), 1)
    padded = jnp.pad(framed, ((0, 0), (0, 0), (1, 1)))
    gpadded = jnp.pad(gframed, ((0, 0), (0, 0), (1, 1)))
    contract_pixels = (((0, 2), (0, 2)), ((), ()))

    band = 3 * channels
    grad_rows = jnp.pad(grad_first, ((2, 0), (0, 0), (0, 0)))
    extended = jnp.concatenate([column_taps(padded, img_width, False), grad_rows], axis=1)
    taps = extended[:, :band]

    def block_of(first, second):
        right = extended if second == 2 else taps
        return lax.dot_general(
            taps[first : first + strip_rows],
            right[second : second + strip_rows],
            contract_pixels,
            preferred_element_type=jnp.float32,
        )

    upper = {(i, j): block_of(i, j) for i in range(3) for j in range(i, 3)}
    cross_part = jnp.concatenate([upper[(i, 2)][:, band:] for i in range(3)], axis=0)
    upper = {key: value[:, :band] for key, value in upper.items()}
    order = sorted(upper)
    paired = jnp.concatenate(
        [jnp.concatenate([upper[order[2 * n]], upper[order[2 * n + 1]]], axis=1) for n in range(3)], axis=0
    )
    row_sums = jnp.sum(taps, axis=2, dtype=jnp.float32)
    patch_part = jnp.concatenate([jnp.sum(row_sums[i : i + strip_rows], axis=0) for i in range(3)])
    grad_part = jnp.sum(grad_first, axis=(0, 2), dtype=jnp.float32)
    grad_column = jnp.zeros((patch_dim,), jnp.float32).at[:channels].set(grad_part)
    lanes = 128
    tail = jnp.concatenate(
        [
            cross_part,
            patch_part[:, None],
            grad_column[:, None],
            jnp.zeros((patch_dim, lanes - channels - 2), jnp.float32),
        ],
        axis=1,
    )
    top = jnp.concatenate([paired, tail], axis=1)
    world = lax.axis_size("dp") * lax.axis_size("rows")
    padded_rows = -(-patch_dim // world) * world
    local = jnp.concatenate([top, jnp.zeros((padded_rows - patch_dim, top.shape[1]), jnp.float32)], axis=0)
    total = tree_psum(local, ("dp", "rows"), physical_levels(world))

    reduced = {}
    for n in range(3):
        for m in range(2):
            reduced[order[2 * n + m]] = total[n * band : (n + 1) * band, m * band : (m + 1) * band]
    gram_whole = jnp.concatenate(
        [
            jnp.concatenate([reduced[(i, j)] if j >= i else reduced[(j, i)].T for j in range(3)], axis=1)
            for i in range(3)
        ],
        axis=0,
    )
    tail_total = total[:patch_dim, 2 * band :]
    cross_total = tail_total[:, :channels]
    patch_sums = tail_total[:, channels]
    grad_sum = tail_total[:channels, channels + 1]

    mean_vec = patch_sums / pixels
    identity = jnp.eye(patch_dim, dtype=jnp.float32)
    covariance = gram_whole / pixels - jnp.outer(mean_vec, mean_vec) + eps_value * identity
    frob_norm = jnp.sqrt(jnp.sum(covariance * covariance))
    iter_y = covariance / frob_norm
    factor = 0.5 * (3.0 * identity - iter_y)
    iter_y = jnp.dot(factor, iter_y, precision=highest)
    iter_z = factor
    for sweep in range(1, ITERS):
        factor = 0.5 * (3.0 * identity - jnp.dot(iter_z, iter_y, precision=highest))
        if sweep < ITERS - 1:
            iter_y = jnp.dot(factor, iter_y, precision=highest)
        iter_z = jnp.dot(factor, iter_z, precision=highest)
    inv_root = iter_z / jnp.sqrt(frob_norm)
    mixing = jnp.dot(inv_root, conv_w, precision=highest)
    mixing_b = mixing.astype(jnp.bfloat16)
    bias_shift = bias - jnp.dot(mean_vec, mixing, precision=highest)
    grad_w = (
        jnp.dot(inv_root.T, cross_total - jnp.outer(mean_vec, grad_sum), precision=highest)
        / pixels
    )
    contract_band = (((0,), (1,)), ((), ()))
    forward_bands = mixing_b.reshape(3, band, channels)
    out_rows = bias_shift[:, None, None]
    for i in range(3):
        out_rows = out_rows + lax.dot_general(
            forward_bands[i], taps[i : i + strip_rows], contract_band, preferred_element_type=jnp.float32
        )
    out_buffer = out_rows.astype(jnp.bfloat16)
    gtaps = column_taps(gpadded, img_width, True)
    flipped = mixing_b.reshape(3, 3, channels, channels)[::-1]
    back_bands = flipped.transpose(0, 2, 1, 3).reshape(3, channels, band)
    contract_back = (((1,), (1,)), ((), ()))
    back_rows = None
    for i in range(3):
        term = lax.dot_general(
            back_bands[i], gtaps[i : i + strip_rows], contract_back, preferred_element_type=jnp.float32
        )
        back_rows = term if back_rows is None else back_rows + term
    back_buffer = back_rows.astype(jnp.bfloat16)
    return (out_buffer[None], back_buffer[None], grad_w)


def solution(mesh):
    placed = (P("dp", None, "rows", None), P(), P(), P("dp", None, "rows", None))
    return jax.shard_map(
        on_device,
        mesh=mesh,
        in_specs=placed,
        out_specs=(P("dp", None, "rows", None), P("dp", None, "rows", None), P()),
        check_vma=False,
    )
```

```python
import jax
import jax.numpy as jnp
from jax import lax
from jax.sharding import PartitionSpec as P

ITERS = 5


eps_value = 1e-05


def with_halo(block, sides, width):
    for axis, dim in sides:
        count = lax.axis_size(axis)
        forward = [(i, i + 1) for i in range(count - 1)]
        backward = [(target, source) for source, target in forward]
        low = lax.ppermute(
            lax.slice_in_dim(block, block.shape[dim] - width, None, axis=dim), axis, forward
        )
        high = lax.ppermute(lax.slice_in_dim(block, 0, width, axis=dim), axis, backward)
        block = jnp.concatenate([low, block, high], axis=dim)
    return block


def column_taps(padded, img_width, flipped):
    order = (2, 1, 0) if flipped else (0, 1, 2)
    return jnp.concatenate([padded[:, :, first : first + img_width] for first in order], axis=1)


def tree_psum(block, axes, levels):
    size = 1
    for axis in axes:
        size *= lax.axis_size(axis)
    index = 0
    for axis in axes:
        index = index * lax.axis_size(axis) + lax.axis_index(axis)
    trail = []
    for stride, radix in levels:
        digit = (index // stride) % radix
        parts = block.reshape((radix, block.shape[0] // radix) + block.shape[1:])
        block = lax.dynamic_index_in_dim(parts, digit, 0, keepdims=False)
        shifts = []
        for shift in range(1, radix):
            pairs = [
                (i, i + ((((i // stride) % radix) + shift) % radix - (i // stride) % radix) * stride)
                for i in range(size)
            ]
            send = lax.dynamic_index_in_dim(parts, (digit + shift) % radix, 0, keepdims=False)
            block = block + lax.ppermute(send, axes, pairs)
            shifts.append(pairs)
        trail.append((radix, digit, shifts))
    for radix, digit, shifts in reversed(trail):
        pieces = [block] + [lax.ppermute(block, axes, pairs) for pairs in shifts]
        placed = []
        for position in range(radix):
            source = (digit - position) % radix
            value = pieces[0]
            for shift in range(1, radix):
                value = jnp.where(source == shift, pieces[shift], value)
            placed.append(value)
        block = jnp.concatenate(placed, axis=0)
    return block


def physical_levels(mesh_sizes):
    levels, stride, rest = [], 1, mesh_sizes
    if rest % 2 == 0 and rest > 2 and ((rest // 2) & (rest // 2 - 1)) == 0 and (rest // 2).bit_length() % 2 == 1:
        levels.append((1, 2))
        stride, rest = 2, rest // 2
    while rest % 4 == 0:
        levels.append((stride, 4))
        stride, rest = stride * 4, rest // 4
    while rest % 2 == 0:
        levels.append((stride, 2))
        stride, rest = stride * 2, rest // 2
    return levels


def on_device(images, conv_w, bias, cotangent):
    highest = lax.Precision.HIGHEST
    channels = images.shape[1]
    strip_rows = images.shape[2]
    img_width = images.shape[3]
    patch_dim = 9 * channels
    pixels = images.shape[0] * strip_rows * img_width * lax.axis_size("rows") * lax.axis_size("dp")
    rows_first = images[0].transpose(1, 0, 2)
    grad_first = cotangent[0].transpose(1, 0, 2)
    framed = with_halo(rows_first, (("rows", 0),), 1)
    gframed = with_halo(grad_first, (("rows", 0),), 1)
    padded = jnp.pad(framed, ((0, 0), (0, 0), (1, 1)))
    gpadded = jnp.pad(gframed, ((0, 0), (0, 0), (1, 1)))
    contract_pixels = (((0, 2), (0, 2)), ((), ()))

    taps = column_taps(padded, img_width, False)
    band = 3 * channels

    def block_of(first, second):
        return lax.dot_general(
            taps[first : first + strip_rows],
            taps[second : second + strip_rows],
            contract_pixels,
            preferred_element_type=jnp.float32,
        )

    upper = {(i, j): block_of(i, j) for i in range(3) for j in range(i, 3)}
    order = sorted(upper)
    paired = jnp.concatenate(
        [jnp.concatenate([upper[order[2 * n]], upper[order[2 * n + 1]]], axis=1) for n in range(3)], axis=0
    )
    cross_part = jnp.concatenate(
        [
            lax.dot_general(
                taps[i : i + strip_rows], grad_first, contract_pixels, preferred_element_type=jnp.float32
            )
            for i in range(3)
        ],
        axis=0,
    )
    row_sums = jnp.sum(taps, axis=2, dtype=jnp.float32)
    patch_part = jnp.concatenate([jnp.sum(row_sums[i : i + strip_rows], axis=0) for i in range(3)])
    grad_part = jnp.sum(grad_first, axis=(0, 2), dtype=jnp.float32)
    grad_column = jnp.zeros((patch_dim,), jnp.float32).at[:channels].set(grad_part)
    lanes = 128
    tail = jnp.concatenate(
        [
            cross_part,
            patch_part[:, None],
            grad_column[:, None],
            jnp.zeros((patch_dim, lanes - channels - 2), jnp.float32),
        ],
        axis=1,
    )
    top = jnp.concatenate([paired, tail], axis=1)
    world = lax.axis_size("dp") * lax.axis_size("rows")
    padded_rows = -(-patch_dim // world) * world
    local = jnp.concatenate([top, jnp.zeros((padded_rows - patch_dim, top.shape[1]), jnp.float32)], axis=0)
    total = tree_psum(local, ("dp", "rows"), physical_levels(world))

    reduced = {}
    for n in range(3):
        for m in range(2):
            reduced[order[2 * n + m]] = total[n * band : (n + 1) * band, m * band : (m + 1) * band]
    gram_whole = jnp.concatenate(
        [
            jnp.concatenate([reduced[(i, j)] if j >= i else reduced[(j, i)].T for j in range(3)], axis=1)
            for i in range(3)
        ],
        axis=0,
    )
    tail_total = total[:patch_dim, 2 * band :]
    cross_total = tail_total[:, :channels]
    patch_sums = tail_total[:, channels]
    grad_sum = tail_total[:channels, channels + 1]

    mean_vec = patch_sums / pixels
    identity = jnp.eye(patch_dim, dtype=jnp.float32)
    covariance = gram_whole / pixels - jnp.outer(mean_vec, mean_vec) + eps_value * identity
    frob_norm = jnp.sqrt(jnp.sum(covariance * covariance))
    iter_y = covariance / frob_norm
    factor = 0.5 * (3.0 * identity - iter_y)
    iter_y = jnp.dot(factor, iter_y, precision=highest)
    iter_z = factor
    for sweep in range(1, ITERS):
        factor = 0.5 * (3.0 * identity - jnp.dot(iter_z, iter_y, precision=highest))
        if sweep < ITERS - 1:
            iter_y = jnp.dot(factor, iter_y, precision=highest)
        iter_z = jnp.dot(factor, iter_z, precision=highest)
    inv_root = iter_z / jnp.sqrt(frob_norm)
    mixing = jnp.dot(inv_root, conv_w, precision=highest)
    mixing_b = mixing.astype(jnp.bfloat16)
    bias_shift = bias - jnp.dot(mean_vec, mixing, precision=highest)
    grad_w = (
        jnp.dot(inv_root.T, cross_total - jnp.outer(mean_vec, grad_sum), precision=highest)
        / pixels
    )
    contract_first = (((0,), (0,)), ((), ()))
    out_rows = []
    for h in range(strip_rows):
        row = lax.dot_general(
            mixing_b,
            taps[h : h + 3].reshape(patch_dim, img_width),
            contract_first,
            preferred_element_type=jnp.float32,
        )
        out_rows.append((row + bias_shift[:, None]).astype(jnp.bfloat16))
    out_buffer = jnp.stack(out_rows, axis=1)
    gtaps = column_taps(gpadded, img_width, True)
    flipped = mixing_b.reshape(3, 3, channels, channels)[::-1]
    back_w = flipped.transpose(2, 0, 1, 3).reshape(channels, patch_dim)
    back_rows = []
    for h in range(strip_rows):
        row = jnp.dot(
            back_w, gtaps[h : h + 3].reshape(patch_dim, img_width), preferred_element_type=jnp.float32
        )
        back_rows.append(row.astype(jnp.bfloat16))
    back_buffer = jnp.stack(back_rows, axis=1)
    return (out_buffer[None], back_buffer[None], grad_w)


def solution(mesh):
    placed = (P("dp", None, "rows", None), P(), P(), P("dp", None, "rows", None))
    return jax.shard_map(
        on_device,
        mesh=mesh,
        in_specs=placed,
        out_specs=(P("dp", None, "rows", None), P("dp", None, "rows", None), P()),
        check_vma=False,
    )
```

```python
import jax
import jax.numpy as jnp
from jax import lax
from jax.experimental import pallas as pl
from jax.sharding import PartitionSpec as P

ITERS = 5


eps_value = 1e-05


def with_halo(block, sides, width):
    for axis, dim in sides:
        count = lax.axis_size(axis)
        forward = [(i, i + 1) for i in range(count - 1)]
        backward = [(target, source) for source, target in forward]
        low = lax.ppermute(
            lax.slice_in_dim(block, block.shape[dim] - width, None, axis=dim), axis, forward
        )
        high = lax.ppermute(lax.slice_in_dim(block, 0, width, axis=dim), axis, backward)
        block = jnp.concatenate([low, block, high], axis=dim)
    return block


def column_taps(padded, img_width, flipped):
    order = (2, 1, 0) if flipped else (0, 1, 2)
    return jnp.concatenate([padded[:, :, first : first + img_width] for first in order], axis=1)


def tree_psum(block, axes, levels):
    size = 1
    for axis in axes:
        size *= lax.axis_size(axis)
    index = 0
    for axis in axes:
        index = index * lax.axis_size(axis) + lax.axis_index(axis)
    trail = []
    for stride, radix in levels:
        digit = (index // stride) % radix
        parts = block.reshape((radix, block.shape[0] // radix) + block.shape[1:])
        block = lax.dynamic_index_in_dim(parts, digit, 0, keepdims=False)
        shifts = []
        for shift in range(1, radix):
            pairs = [
                (i, i + ((((i // stride) % radix) + shift) % radix - (i // stride) % radix) * stride)
                for i in range(size)
            ]
            send = lax.dynamic_index_in_dim(parts, (digit + shift) % radix, 0, keepdims=False)
            block = block + lax.ppermute(send, axes, pairs)
            shifts.append(pairs)
        trail.append((radix, digit, shifts))
    for radix, digit, shifts in reversed(trail):
        pieces = [block] + [lax.ppermute(block, axes, pairs) for pairs in shifts]
        placed = []
        for position in range(radix):
            source = (digit - position) % radix
            value = pieces[0]
            for shift in range(1, radix):
                value = jnp.where(source == shift, pieces[shift], value)
            placed.append(value)
        block = jnp.concatenate(placed, axis=0)
    return block


def physical_levels(mesh_sizes):
    levels, stride, rest = [], 1, mesh_sizes
    if rest % 2 == 0 and rest > 2 and ((rest // 2) & (rest // 2 - 1)) == 0 and (rest // 2).bit_length() % 2 == 1:
        levels.append((1, 2))
        stride, rest = 2, rest // 2
    while rest % 4 == 0:
        levels.append((stride, 4))
        stride, rest = stride * 4, rest // 4
    while rest % 2 == 0:
        levels.append((stride, 2))
        stride, rest = stride * 2, rest // 2
    return levels


def rows_kernel(fw_ref, bias_ref, taps_ref, bw_ref, gtaps_ref, out_ref, back_ref):
    for h in range(out_ref.shape[0]):
        acc = bias_ref[...]
        back = None
        for i in range(3):
            acc = acc + jnp.dot(fw_ref[i], taps_ref[h + i], preferred_element_type=jnp.float32)
            term = jnp.dot(bw_ref[i], gtaps_ref[h + i], preferred_element_type=jnp.float32)
            back = term if back is None else back + term
        out_ref[h] = acc.astype(out_ref.dtype)
        back_ref[h] = back.astype(back_ref.dtype)


def on_device(images, conv_w, bias, cotangent):
    highest = lax.Precision.HIGHEST
    channels = images.shape[1]
    strip_rows = images.shape[2]
    img_width = images.shape[3]
    patch_dim = 9 * channels
    pixels = images.shape[0] * strip_rows * img_width * lax.axis_size("rows") * lax.axis_size("dp")
    rows_first = images[0].transpose(1, 0, 2)
    grad_first = cotangent[0].transpose(1, 0, 2)
    framed = with_halo(rows_first, (("rows", 0),), 1)
    gframed = with_halo(grad_first, (("rows", 0),), 1)
    padded = jnp.pad(framed, ((0, 0), (0, 0), (1, 1)))
    gpadded = jnp.pad(gframed, ((0, 0), (0, 0), (1, 1)))
    contract_pixels = (((0, 2), (0, 2)), ((), ()))

    taps = column_taps(padded, img_width, False)
    band = 3 * channels

    def block_of(first, second):
        return lax.dot_general(
            taps[first : first + strip_rows],
            taps[second : second + strip_rows],
            contract_pixels,
            preferred_element_type=jnp.float32,
        )

    upper = {(i, j): block_of(i, j) for i in range(3) for j in range(i, 3)}
    order = sorted(upper)
    paired = jnp.concatenate(
        [jnp.concatenate([upper[order[2 * n]], upper[order[2 * n + 1]]], axis=1) for n in range(3)], axis=0
    )
    cross_part = jnp.concatenate(
        [
            lax.dot_general(
                taps[i : i + strip_rows], grad_first, contract_pixels, preferred_element_type=jnp.float32
            )
            for i in range(3)
        ],
        axis=0,
    )
    row_sums = jnp.sum(taps, axis=2, dtype=jnp.float32)
    patch_part = jnp.concatenate([jnp.sum(row_sums[i : i + strip_rows], axis=0) for i in range(3)])
    grad_part = jnp.sum(grad_first, axis=(0, 2), dtype=jnp.float32)
    grad_column = jnp.zeros((patch_dim,), jnp.float32).at[:channels].set(grad_part)
    lanes = 128
    tail = jnp.concatenate(
        [
            cross_part,
            patch_part[:, None],
            grad_column[:, None],
            jnp.zeros((patch_dim, lanes - channels - 2), jnp.float32),
        ],
        axis=1,
    )
    top = jnp.concatenate([paired, tail], axis=1)
    world = lax.axis_size("dp") * lax.axis_size("rows")
    padded_rows = -(-patch_dim // world) * world
    local = jnp.concatenate([top, jnp.zeros((padded_rows - patch_dim, top.shape[1]), jnp.float32)], axis=0)
    total = tree_psum(local, ("dp", "rows"), physical_levels(world))

    reduced = {}
    for n in range(3):
        for m in range(2):
            reduced[order[2 * n + m]] = total[n * band : (n + 1) * band, m * band : (m + 1) * band]
    gram_whole = jnp.concatenate(
        [
            jnp.concatenate([reduced[(i, j)] if j >= i else reduced[(j, i)].T for j in range(3)], axis=1)
            for i in range(3)
        ],
        axis=0,
    )
    tail_total = total[:patch_dim, 2 * band :]
    cross_total = tail_total[:, :channels]
    patch_sums = tail_total[:, channels]
    grad_sum = tail_total[:channels, channels + 1]

    mean_vec = patch_sums / pixels
    identity = jnp.eye(patch_dim, dtype=jnp.float32)
    covariance = gram_whole / pixels - jnp.outer(mean_vec, mean_vec) + eps_value * identity
    frob_norm = jnp.sqrt(jnp.sum(covariance * covariance))
    iter_y = covariance / frob_norm
    factor = 0.5 * (3.0 * identity - iter_y)
    iter_y = jnp.dot(factor, iter_y, precision=highest)
    iter_z = factor
    for sweep in range(1, ITERS):
        factor = 0.5 * (3.0 * identity - jnp.dot(iter_z, iter_y, precision=highest))
        if sweep < ITERS - 1:
            iter_y = jnp.dot(factor, iter_y, precision=highest)
        iter_z = jnp.dot(factor, iter_z, precision=highest)
    inv_root = iter_z / jnp.sqrt(frob_norm)
    mixing = jnp.dot(inv_root, conv_w, precision=highest)
    mixing_b = mixing.astype(jnp.bfloat16)
    bias_shift = bias - jnp.dot(mean_vec, mixing, precision=highest)
    grad_w = (
        jnp.dot(inv_root.T, cross_total - jnp.outer(mean_vec, grad_sum), precision=highest)
        / pixels
    )
    forward_bands = mixing_b.reshape(3, band, channels).transpose(0, 2, 1)
    gtaps = column_taps(gpadded, img_width, True)
    flipped = mixing_b.reshape(3, 3, channels, channels)[::-1]
    back_bands = flipped.transpose(0, 2, 1, 3).reshape(3, channels, band)
    row_major = jax.ShapeDtypeStruct((strip_rows, channels, img_width), jnp.bfloat16)
    out_rows, back_rows = pl.pallas_call(rows_kernel, out_shape=(row_major, row_major))(
        forward_bands, bias_shift[:, None], taps, back_bands, gtaps
    )
    out_buffer = out_rows.transpose(1, 0, 2)
    back_buffer = back_rows.transpose(1, 0, 2)
    return (out_buffer[None], back_buffer[None], grad_w)


def solution(mesh):
    placed = (P("dp", None, "rows", None), P(), P(), P("dp", None, "rows", None))
    return jax.shard_map(
        on_device,
        mesh=mesh,
        in_specs=placed,
        out_specs=(P("dp", None, "rows", None), P("dp", None, "rows", None), P()),
        check_vma=False,
    )
```

```python
import jax
import jax.numpy as jnp
from jax import lax
from jax.experimental import pallas as pl
from jax.sharding import PartitionSpec as P

ITERS = 5


eps_value = 1e-05


def with_halo(block, sides, width):
    for axis, dim in sides:
        count = lax.axis_size(axis)
        forward = [(i, i + 1) for i in range(count - 1)]
        backward = [(target, source) for source, target in forward]
        low = lax.ppermute(
            lax.slice_in_dim(block, block.shape[dim] - width, None, axis=dim), axis, forward
        )
        high = lax.ppermute(lax.slice_in_dim(block, 0, width, axis=dim), axis, backward)
        block = jnp.concatenate([low, block, high], axis=dim)
    return block


def column_taps(padded, img_width, flipped):
    order = (2, 1, 0) if flipped else (0, 1, 2)
    return jnp.concatenate([padded[:, :, first : first + img_width] for first in order], axis=1)


def tree_psum(block, axes, levels):
    size = 1
    for axis in axes:
        size *= lax.axis_size(axis)
    index = 0
    for axis in axes:
        index = index * lax.axis_size(axis) + lax.axis_index(axis)
    trail = []
    for stride, radix in levels:
        digit = (index // stride) % radix
        parts = block.reshape((radix, block.shape[0] // radix) + block.shape[1:])
        block = lax.dynamic_index_in_dim(parts, digit, 0, keepdims=False)
        shifts = []
        for shift in range(1, radix):
            pairs = [
                (i, i + ((((i // stride) % radix) + shift) % radix - (i // stride) % radix) * stride)
                for i in range(size)
            ]
            send = lax.dynamic_index_in_dim(parts, (digit + shift) % radix, 0, keepdims=False)
            block = block + lax.ppermute(send, axes, pairs)
            shifts.append(pairs)
        trail.append((radix, digit, shifts))
    for radix, digit, shifts in reversed(trail):
        pieces = [block] + [lax.ppermute(block, axes, pairs) for pairs in shifts]
        placed = []
        for position in range(radix):
            source = (digit - position) % radix
            value = pieces[0]
            for shift in range(1, radix):
                value = jnp.where(source == shift, pieces[shift], value)
            placed.append(value)
        block = jnp.concatenate(placed, axis=0)
    return block


def physical_levels(mesh_sizes):
    levels, stride, rest = [], 1, mesh_sizes
    if rest % 2 == 0 and rest > 2 and ((rest // 2) & (rest // 2 - 1)) == 0 and (rest // 2).bit_length() % 2 == 1:
        levels.append((1, 2))
        stride, rest = 2, rest // 2
    while rest % 4 == 0:
        levels.append((stride, 4))
        stride, rest = stride * 4, rest // 4
    while rest % 2 == 0:
        levels.append((stride, 2))
        stride, rest = stride * 2, rest // 2
    return levels


def rows_kernel(fw_ref, bias_ref, taps_ref, bw_ref, gtaps_ref, out_ref, back_ref):
    for h in range(out_ref.shape[1]):
        acc = bias_ref[...]
        back = None
        for i in range(3):
            acc = acc + jnp.dot(fw_ref[i], taps_ref[h + i], preferred_element_type=jnp.float32)
            term = jnp.dot(bw_ref[i], gtaps_ref[h + i], preferred_element_type=jnp.float32)
            back = term if back is None else back + term
        out_ref[:, h, :] = acc.astype(out_ref.dtype)
        back_ref[:, h, :] = back.astype(back_ref.dtype)


def on_device(images, conv_w, bias, cotangent):
    highest = lax.Precision.HIGHEST
    channels = images.shape[1]
    strip_rows = images.shape[2]
    img_width = images.shape[3]
    patch_dim = 9 * channels
    pixels = images.shape[0] * strip_rows * img_width * lax.axis_size("rows") * lax.axis_size("dp")
    rows_first = images[0].transpose(1, 0, 2)
    grad_first = cotangent[0].transpose(1, 0, 2)
    framed = with_halo(rows_first, (("rows", 0),), 1)
    gframed = with_halo(grad_first, (("rows", 0),), 1)
    padded = jnp.pad(framed, ((0, 0), (0, 0), (1, 1)))
    gpadded = jnp.pad(gframed, ((0, 0), (0, 0), (1, 1)))
    contract_pixels = (((0, 2), (0, 2)), ((), ()))

    taps = column_taps(padded, img_width, False)
    band = 3 * channels

    def block_of(first, second):
        return lax.dot_general(
            taps[first : first + strip_rows],
            taps[second : second + strip_rows],
            contract_pixels,
            preferred_element_type=jnp.float32,
        )

    upper = {(i, j): block_of(i, j) for i in range(3) for j in range(i, 3)}
    order = sorted(upper)
    paired = jnp.concatenate(
        [jnp.concatenate([upper[order[2 * n]], upper[order[2 * n + 1]]], axis=1) for n in range(3)], axis=0
    )
    cross_part = jnp.concatenate(
        [
            lax.dot_general(
                taps[i : i + strip_rows], grad_first, contract_pixels, preferred_element_type=jnp.float32
            )
            for i in range(3)
        ],
        axis=0,
    )
    row_sums = jnp.sum(taps, axis=2, dtype=jnp.float32)
    patch_part = jnp.concatenate([jnp.sum(row_sums[i : i + strip_rows], axis=0) for i in range(3)])
    grad_part = jnp.sum(grad_first, axis=(0, 2), dtype=jnp.float32)
    grad_column = jnp.zeros((patch_dim,), jnp.float32).at[:channels].set(grad_part)
    lanes = 128
    tail = jnp.concatenate(
        [
            cross_part,
            patch_part[:, None],
            grad_column[:, None],
            jnp.zeros((patch_dim, lanes - channels - 2), jnp.float32),
        ],
        axis=1,
    )
    top = jnp.concatenate([paired, tail], axis=1)
    world = lax.axis_size("dp") * lax.axis_size("rows")
    padded_rows = -(-patch_dim // world) * world
    local = jnp.concatenate([top, jnp.zeros((padded_rows - patch_dim, top.shape[1]), jnp.float32)], axis=0)
    total = tree_psum(local, ("dp", "rows"), physical_levels(world))

    reduced = {}
    for n in range(3):
        for m in range(2):
            reduced[order[2 * n + m]] = total[n * band : (n + 1) * band, m * band : (m + 1) * band]
    gram_whole = jnp.concatenate(
        [
            jnp.concatenate([reduced[(i, j)] if j >= i else reduced[(j, i)].T for j in range(3)], axis=1)
            for i in range(3)
        ],
        axis=0,
    )
    tail_total = total[:patch_dim, 2 * band :]
    cross_total = tail_total[:, :channels]
    patch_sums = tail_total[:, channels]
    grad_sum = tail_total[:channels, channels + 1]

    mean_vec = patch_sums / pixels
    identity = jnp.eye(patch_dim, dtype=jnp.float32)
    covariance = gram_whole / pixels - jnp.outer(mean_vec, mean_vec) + eps_value * identity
    frob_norm = jnp.sqrt(jnp.sum(covariance * covariance))
    iter_y = covariance / frob_norm
    factor = 0.5 * (3.0 * identity - iter_y)
    iter_y = jnp.dot(factor, iter_y, precision=highest)
    iter_z = factor
    for sweep in range(1, ITERS):
        factor = 0.5 * (3.0 * identity - jnp.dot(iter_z, iter_y, precision=highest))
        if sweep < ITERS - 1:
            iter_y = jnp.dot(factor, iter_y, precision=highest)
        iter_z = jnp.dot(factor, iter_z, precision=highest)
    inv_root = iter_z / jnp.sqrt(frob_norm)
    mixing = jnp.dot(inv_root, conv_w, precision=highest)
    mixing_b = mixing.astype(jnp.bfloat16)
    bias_shift = bias - jnp.dot(mean_vec, mixing, precision=highest)
    grad_w = (
        jnp.dot(inv_root.T, cross_total - jnp.outer(mean_vec, grad_sum), precision=highest)
        / pixels
    )
    forward_bands = mixing_b.reshape(3, band, channels).transpose(0, 2, 1)
    gtaps = column_taps(gpadded, img_width, True)
    flipped = mixing_b.reshape(3, 3, channels, channels)[::-1]
    back_bands = flipped.transpose(0, 2, 1, 3).reshape(3, channels, band)
    channel_major = jax.ShapeDtypeStruct((channels, strip_rows, img_width), jnp.bfloat16)
    out_buffer, back_buffer = pl.pallas_call(rows_kernel, out_shape=(channel_major, channel_major))(
        forward_bands, bias_shift[:, None], taps, back_bands, gtaps
    )
    return (out_buffer[None], back_buffer[None], grad_w)


def solution(mesh):
    placed = (P("dp", None, "rows", None), P(), P(), P("dp", None, "rows", None))
    return jax.shard_map(
        on_device,
        mesh=mesh,
        in_specs=placed,
        out_specs=(P("dp", None, "rows", None), P("dp", None, "rows", None), P()),
        check_vma=False,
    )
```

```python
import jax
import jax.numpy as jnp
from jax import lax
from jax.experimental import pallas as pl
from jax.sharding import PartitionSpec as P

ITERS = 5


eps_value = 1e-05


def with_halo(block, sides, width):
    for axis, dim in sides:
        count = lax.axis_size(axis)
        forward = [(i, i + 1) for i in range(count - 1)]
        backward = [(target, source) for source, target in forward]
        low = lax.ppermute(
            lax.slice_in_dim(block, block.shape[dim] - width, None, axis=dim), axis, forward
        )
        high = lax.ppermute(lax.slice_in_dim(block, 0, width, axis=dim), axis, backward)
        block = jnp.concatenate([low, block, high], axis=dim)
    return block


def column_taps(padded, img_width, flipped):
    order = (2, 1, 0) if flipped else (0, 1, 2)
    return jnp.concatenate([padded[:, :, first : first + img_width] for first in order], axis=1)


def tree_psum(block, axes, levels):
    size = 1
    for axis in axes:
        size *= lax.axis_size(axis)
    index = 0
    for axis in axes:
        index = index * lax.axis_size(axis) + lax.axis_index(axis)
    trail = []
    for stride, radix in levels:
        digit = (index // stride) % radix
        parts = block.reshape((radix, block.shape[0] // radix) + block.shape[1:])
        block = lax.dynamic_index_in_dim(parts, digit, 0, keepdims=False)
        shifts = []
        for shift in range(1, radix):
            pairs = [
                (i, i + ((((i // stride) % radix) + shift) % radix - (i // stride) % radix) * stride)
                for i in range(size)
            ]
            send = lax.dynamic_index_in_dim(parts, (digit + shift) % radix, 0, keepdims=False)
            block = block + lax.ppermute(send, axes, pairs)
            shifts.append(pairs)
        trail.append((radix, digit, shifts))
    for radix, digit, shifts in reversed(trail):
        pieces = [block] + [lax.ppermute(block, axes, pairs) for pairs in shifts]
        placed = []
        for position in range(radix):
            source = (digit - position) % radix
            value = pieces[0]
            for shift in range(1, radix):
                value = jnp.where(source == shift, pieces[shift], value)
            placed.append(value)
        block = jnp.concatenate(placed, axis=0)
    return block


def physical_levels(mesh_sizes):
    levels, stride, rest = [], 1, mesh_sizes
    if rest % 2 == 0 and rest > 2 and ((rest // 2) & (rest // 2 - 1)) == 0 and (rest // 2).bit_length() % 2 == 1:
        levels.append((1, 2))
        stride, rest = 2, rest // 2
    while rest % 4 == 0:
        levels.append((stride, 4))
        stride, rest = stride * 4, rest // 4
    while rest % 2 == 0:
        levels.append((stride, 2))
        stride, rest = stride * 2, rest // 2
    return levels


def rows_kernel(fw_ref, bias_ref, taps_ref, bw_ref, gtaps_ref, out_ref, back_ref):
    for h in range(out_ref.shape[1]):
        acc = bias_ref[...]
        back = None
        for i in range(3):
            acc = acc + jnp.dot(fw_ref[i], taps_ref[h + i], preferred_element_type=jnp.float32)
            term = jnp.dot(bw_ref[i], gtaps_ref[h + i], preferred_element_type=jnp.float32)
            back = term if back is None else back + term
        out_ref[:, h, :] = acc.astype(out_ref.dtype)
        back_ref[:, h, :] = back.astype(back_ref.dtype)


def on_device(images, conv_w, bias, cotangent):
    highest = lax.Precision.HIGHEST
    channels = images.shape[1]
    strip_rows = images.shape[2]
    img_width = images.shape[3]
    patch_dim = 9 * channels
    pixels = images.shape[0] * strip_rows * img_width * lax.axis_size("rows") * lax.axis_size("dp")
    rows_first = images[0].transpose(1, 0, 2)
    grad_first = cotangent[0].transpose(1, 0, 2)
    framed = with_halo(rows_first, (("rows", 0),), 1)
    gframed = with_halo(grad_first, (("rows", 0),), 1)
    padded = jnp.pad(framed, ((0, 0), (0, 0), (1, 1)))
    gpadded = jnp.pad(gframed, ((0, 0), (0, 0), (1, 1)))
    contract_pixels = (((0, 2), (0, 2)), ((), ()))

    taps = column_taps(padded, img_width, False)
    band = 3 * channels

    def block_of(first, second):
        return lax.dot_general(
            taps[first : first + strip_rows],
            taps[second : second + strip_rows],
            contract_pixels,
            preferred_element_type=jnp.float32,
        )

    upper = {(i, j): block_of(i, j) for i in range(3) for j in range(i, 3)}
    order = sorted(upper)
    paired = jnp.concatenate(
        [jnp.concatenate([upper[order[2 * n]], upper[order[2 * n + 1]]], axis=1) for n in range(3)], axis=0
    )
    cross_part = jnp.concatenate(
        [
            lax.dot_general(
                taps[i : i + strip_rows], grad_first, contract_pixels, preferred_element_type=jnp.float32
            )
            for i in range(3)
        ],
        axis=0,
    )
    row_sums = jnp.sum(taps, axis=2, dtype=jnp.float32)
    patch_part = jnp.concatenate([jnp.sum(row_sums[i : i + strip_rows], axis=0) for i in range(3)])
    grad_part = jnp.sum(grad_first, axis=(0, 2), dtype=jnp.float32)
    grad_column = jnp.zeros((patch_dim,), jnp.float32).at[:channels].set(grad_part)
    lanes = 128
    tail = jnp.concatenate(
        [
            cross_part,
            patch_part[:, None],
            grad_column[:, None],
            jnp.zeros((patch_dim, lanes - channels - 2), jnp.float32),
        ],
        axis=1,
    )
    top = jnp.concatenate([paired, tail], axis=1)
    world = lax.axis_size("dp") * lax.axis_size("rows")
    padded_rows = -(-patch_dim // world) * world
    local = jnp.concatenate([top, jnp.zeros((padded_rows - patch_dim, top.shape[1]), jnp.float32)], axis=0)
    total = tree_psum(local, ("dp", "rows"), physical_levels(world))

    reduced = {}
    for n in range(3):
        for m in range(2):
            reduced[order[2 * n + m]] = total[n * band : (n + 1) * band, m * band : (m + 1) * band]
    gram_whole = jnp.concatenate(
        [
            jnp.concatenate([reduced[(i, j)] if j >= i else reduced[(j, i)].T for j in range(3)], axis=1)
            for i in range(3)
        ],
        axis=0,
    )
    tail_total = total[:patch_dim, 2 * band :]
    cross_total = tail_total[:, :channels]
    patch_sums = tail_total[:, channels]
    grad_sum = tail_total[:channels, channels + 1]

    mean_vec = patch_sums / pixels
    identity = jnp.eye(patch_dim, dtype=jnp.float32)
    covariance = gram_whole / pixels - jnp.outer(mean_vec, mean_vec) + eps_value * identity
    frob_norm = jnp.sqrt(jnp.sum(covariance * covariance))
    iter_y = covariance / frob_norm
    factor = 0.5 * (3.0 * identity - iter_y)
    iter_y = jnp.dot(factor, iter_y, precision=highest)
    iter_z = factor
    for sweep in range(1, ITERS):
        factor = 0.5 * (3.0 * identity - jnp.dot(iter_z, iter_y, precision=highest))
        if sweep < ITERS - 1:
            both = jnp.dot(factor, jnp.concatenate([iter_y, iter_z], axis=1), precision=highest)
            iter_y, iter_z = both[:, :patch_dim], both[:, patch_dim:]
        else:
            iter_z = jnp.dot(factor, iter_z, precision=highest)
    inv_root = iter_z / jnp.sqrt(frob_norm)
    mixing = jnp.dot(inv_root, conv_w, precision=highest)
    mixing_b = mixing.astype(jnp.bfloat16)
    bias_shift = bias - jnp.dot(mean_vec, mixing, precision=highest)
    grad_w = (
        jnp.dot(inv_root.T, cross_total - jnp.outer(mean_vec, grad_sum), precision=highest)
        / pixels
    )
    forward_bands = mixing_b.reshape(3, band, channels).transpose(0, 2, 1)
    gtaps = column_taps(gpadded, img_width, True)
    flipped = mixing_b.reshape(3, 3, channels, channels)[::-1]
    back_bands = flipped.transpose(0, 2, 1, 3).reshape(3, channels, band)
    channel_major = jax.ShapeDtypeStruct((channels, strip_rows, img_width), jnp.bfloat16)
    out_buffer, back_buffer = pl.pallas_call(rows_kernel, out_shape=(channel_major, channel_major))(
        forward_bands, bias_shift[:, None], taps, back_bands, gtaps
    )
    return (out_buffer[None], back_buffer[None], grad_w)


def solution(mesh):
    placed = (P("dp", None, "rows", None), P(), P(), P("dp", None, "rows", None))
    return jax.shard_map(
        on_device,
        mesh=mesh,
        in_specs=placed,
        out_specs=(P("dp", None, "rows", None), P("dp", None, "rows", None), P()),
        check_vma=False,
    )
```

```python
import jax
import jax.numpy as jnp
from jax import lax
from jax.experimental import pallas as pl
from jax.sharding import PartitionSpec as P

ITERS = 5


eps_value = 1e-05


def with_halo(block, sides, width):
    for axis, dim in sides:
        count = lax.axis_size(axis)
        forward = [(i, i + 1) for i in range(count - 1)]
        backward = [(target, source) for source, target in forward]
        low = lax.ppermute(
            lax.slice_in_dim(block, block.shape[dim] - width, None, axis=dim), axis, forward
        )
        high = lax.ppermute(lax.slice_in_dim(block, 0, width, axis=dim), axis, backward)
        block = jnp.concatenate([low, block, high], axis=dim)
    return block


def column_taps(padded, img_width, flipped):
    order = (2, 1, 0) if flipped else (0, 1, 2)
    return jnp.concatenate([padded[:, :, first : first + img_width] for first in order], axis=1)


def tree_psum(block, axes, levels, rider):
    size = 1
    for axis in axes:
        size *= lax.axis_size(axis)
    index = 0
    for axis in axes:
        index = index * lax.axis_size(axis) + lax.axis_index(axis)
    trail = []
    for stride, radix in levels:
        digit = (index // stride) % radix
        parts = block.reshape((radix, block.shape[0] // radix) + block.shape[1:])
        block = lax.dynamic_index_in_dim(parts, digit, 0, keepdims=False)
        shifts = []
        for shift in range(1, radix):
            pairs = [
                (i, i + ((((i // stride) % radix) + shift) % radix - (i // stride) % radix) * stride)
                for i in range(size)
            ]
            send = lax.dynamic_index_in_dim(parts, (digit + shift) % radix, 0, keepdims=False)
            block = block + lax.ppermute(send, axes, pairs)
            shifts.append(pairs)
        trail.append((radix, digit, shifts))
        if len(trail) == 1:
            block, rider = lax.optimization_barrier((block, rider))
    for radix, digit, shifts in reversed(trail):
        pieces = [block] + [lax.ppermute(block, axes, pairs) for pairs in shifts]
        placed = []
        for position in range(radix):
            source = (digit - position) % radix
            value = pieces[0]
            for shift in range(1, radix):
                value = jnp.where(source == shift, pieces[shift], value)
            placed.append(value)
        block = jnp.concatenate(placed, axis=0)
    return block, rider


def physical_levels(mesh_sizes):
    levels, stride, rest = [], 1, mesh_sizes
    if rest % 2 == 0 and rest > 2 and ((rest // 2) & (rest // 2 - 1)) == 0 and (rest // 2).bit_length() % 2 == 1:
        levels.append((1, 2))
        stride, rest = 2, rest // 2
    while rest % 4 == 0:
        levels.append((stride, 4))
        stride, rest = stride * 4, rest // 4
    while rest % 2 == 0:
        levels.append((stride, 2))
        stride, rest = stride * 2, rest // 2
    return levels


def rows_kernel(fw_ref, bias_ref, taps_ref, bw_ref, gtaps_ref, out_ref, back_ref):
    for h in range(out_ref.shape[1]):
        acc = bias_ref[...]
        back = None
        for i in range(3):
            acc = acc + jnp.dot(fw_ref[i], taps_ref[h + i], preferred_element_type=jnp.float32)
            term = jnp.dot(bw_ref[i], gtaps_ref[h + i], preferred_element_type=jnp.float32)
            back = term if back is None else back + term
        out_ref[:, h, :] = acc.astype(out_ref.dtype)
        back_ref[:, h, :] = back.astype(back_ref.dtype)


def on_device(images, conv_w, bias, cotangent):
    highest = lax.Precision.HIGHEST
    channels = images.shape[1]
    strip_rows = images.shape[2]
    img_width = images.shape[3]
    patch_dim = 9 * channels
    pixels = images.shape[0] * strip_rows * img_width * lax.axis_size("rows") * lax.axis_size("dp")
    rows_first = images[0].transpose(1, 0, 2)
    grad_first = cotangent[0].transpose(1, 0, 2)
    framed = with_halo(rows_first, (("rows", 0),), 1)
    gframed = with_halo(grad_first, (("rows", 0),), 1)
    padded = jnp.pad(framed, ((0, 0), (0, 0), (1, 1)))
    gpadded = jnp.pad(gframed, ((0, 0), (0, 0), (1, 1)))
    contract_pixels = (((0, 2), (0, 2)), ((), ()))

    taps = column_taps(padded, img_width, False)
    band = 3 * channels

    def block_of(first, second):
        return lax.dot_general(
            taps[first : first + strip_rows],
            taps[second : second + strip_rows],
            contract_pixels,
            preferred_element_type=jnp.float32,
        )

    upper = {(i, j): block_of(i, j) for i in range(3) for j in range(i, 3)}
    order = sorted(upper)
    paired = jnp.concatenate(
        [jnp.concatenate([upper[order[2 * n]], upper[order[2 * n + 1]]], axis=1) for n in range(3)], axis=0
    )
    cross_part = jnp.concatenate(
        [
            lax.dot_general(
                taps[i : i + strip_rows], grad_first, contract_pixels, preferred_element_type=jnp.float32
            )
            for i in range(3)
        ],
        axis=0,
    )
    row_sums = jnp.sum(taps, axis=2, dtype=jnp.float32)
    patch_part = jnp.concatenate([jnp.sum(row_sums[i : i + strip_rows], axis=0) for i in range(3)])
    grad_part = jnp.sum(grad_first, axis=(0, 2), dtype=jnp.float32)
    grad_column = jnp.zeros((patch_dim,), jnp.float32).at[:channels].set(grad_part)
    lanes = 128
    tail = jnp.concatenate(
        [
            cross_part,
            patch_part[:, None],
            grad_column[:, None],
            jnp.zeros((patch_dim, lanes - channels - 2), jnp.float32),
        ],
        axis=1,
    )
    top = jnp.concatenate([paired, tail], axis=1)
    world = lax.axis_size("dp") * lax.axis_size("rows")
    padded_rows = -(-patch_dim // world) * world
    local = jnp.concatenate([top, jnp.zeros((padded_rows - patch_dim, top.shape[1]), jnp.float32)], axis=0)
    gtaps = column_taps(gpadded, img_width, True)
    total, gtaps = tree_psum(local, ("dp", "rows"), physical_levels(world), gtaps)

    reduced = {}
    for n in range(3):
        for m in range(2):
            reduced[order[2 * n + m]] = total[n * band : (n + 1) * band, m * band : (m + 1) * band]
    gram_whole = jnp.concatenate(
        [
            jnp.concatenate([reduced[(i, j)] if j >= i else reduced[(j, i)].T for j in range(3)], axis=1)
            for i in range(3)
        ],
        axis=0,
    )
    tail_total = total[:patch_dim, 2 * band :]
    cross_total = tail_total[:, :channels]
    patch_sums = tail_total[:, channels]
    grad_sum = tail_total[:channels, channels + 1]

    mean_vec = patch_sums / pixels
    identity = jnp.eye(patch_dim, dtype=jnp.float32)
    covariance = gram_whole / pixels - jnp.outer(mean_vec, mean_vec) + eps_value * identity
    frob_norm = jnp.sqrt(jnp.sum(covariance * covariance))
    iter_y = covariance / frob_norm
    factor = 0.5 * (3.0 * identity - iter_y)
    iter_y = jnp.dot(factor, iter_y, precision=highest)
    iter_z = factor
    for sweep in range(1, ITERS):
        factor = 0.5 * (3.0 * identity - jnp.dot(iter_z, iter_y, precision=highest))
        if sweep < ITERS - 1:
            iter_y = jnp.dot(factor, iter_y, precision=highest)
        iter_z = jnp.dot(factor, iter_z, precision=highest)
    inv_root = iter_z / jnp.sqrt(frob_norm)
    mixing = jnp.dot(inv_root, conv_w, precision=highest)
    mixing_b = mixing.astype(jnp.bfloat16)
    bias_shift = bias - jnp.dot(mean_vec, mixing, precision=highest)
    grad_w = (
        jnp.dot(inv_root.T, cross_total - jnp.outer(mean_vec, grad_sum), precision=highest)
        / pixels
    )
    forward_bands = mixing_b.reshape(3, band, channels).transpose(0, 2, 1)
    flipped = mixing_b.reshape(3, 3, channels, channels)[::-1]
    back_bands = flipped.transpose(0, 2, 1, 3).reshape(3, channels, band)
    channel_major = jax.ShapeDtypeStruct((channels, strip_rows, img_width), jnp.bfloat16)
    out_buffer, back_buffer = pl.pallas_call(rows_kernel, out_shape=(channel_major, channel_major))(
        forward_bands, bias_shift[:, None], taps, back_bands, gtaps
    )
    return (out_buffer[None], back_buffer[None], grad_w)


def solution(mesh):
    placed = (P("dp", None, "rows", None), P(), P(), P("dp", None, "rows", None))
    return jax.shard_map(
        on_device,
        mesh=mesh,
        in_specs=placed,
        out_specs=(P("dp", None, "rows", None), P("dp", None, "rows", None), P()),
        check_vma=False,
    )
```
